256 devices in a mesh: kv: 2 (over core), pg: 128 (over x, z, y).
Axes of the slice: x: 4, y: 4, z: 8, core: 2. Of those that a mesh axis runs over, the one named last changes fastest.
Arguments:
- layer_hidden_input: bfloat16 [16384, 2560], P('pg'), may hold values from -6 to 6
- norm_scale_vector: float32 [2560], replicated, may hold values from 0.1 to 1.9
- expert_choice_index: int32 [16384, 6], P('pg'), may hold values from 0 to 63, all different within a row; in each aligned block of 128 rows (0 to 127, 128 to 255, ...) at most 16 rows name the same one
- expert_choice_weight: float32 [16384, 6], P('pg'), may hold values from 0.05 to 0.35
- request_of_token: int32 [16384], P('pg'), may hold values from 0 to 255, never falling along the last dimension, each value on 1 to 512 neighbouring positions
- adapter_of_request: int32 [256], replicated, may hold values from 0 to 63
- adapter_of_slot: int32 [128], replicated, may hold values from 0 to 63, as said below
- expert_gate_up_weight: bfloat16 [128, 2560, 2, 768], P('pg', None, None, 'kv'), may hold values from -0.125 to 0.125
- expert_down_weight: bfloat16 [128, 768, 2560], P('pg', 'kv'), may hold values from -0.15625 to 0.15625
- adapter_down_weight: bfloat16 [128, 2560, 8], P('pg'), may hold values from -0.125 to 0.125
- adapter_up_weight: bfloat16 [128, 8, 2560], P('pg', None, 'kv'), may hold values from -0.75 to 0.75
Outputs:
- mixed: bfloat16 [16384, 2560], P('pg', 'kv')
The draws below stay inside these ranges and needn't reach their ends.
Inputs may be any that keep to these rules, and one draw needn't show every extreme that they name: `expert_choice_index`: each row names 6 different experts. The 128 rows of one index of pg name one expert at most 16 times; some expert is named exactly 16 times by the rows of some index. `adapter_of_slot`: every adapter is held by exactly two slots. `request_of_token`: tokens of one request stand in a row; request numbers never fall along the tokens.
All inputs are finite; a program needn't handle non-finite values.
Results may differ from the reference program's by a relative error of at most 0.013.
Values may be sent and summed in bfloat16 or wider, within the bound.
No kernel may reach another device: no remote copies, remote signals or barrier semaphores. Data moves between devices by JAX's collectives and lax.ppermute only.
A program may use at most 128 MiB of HBM per device.

```python
import math
import jax
import jax.numpy as jnp
import numpy as np
from jax import lax

MODEL_DIM = 2560
FF = 1536
TOP = 6
ADAPTER_RANK = 16
TOK_DEV = 128
EXPERTS = 64
ADAPTER_TOTAL = 64
CAP = 16
TOKENS = 16384
REQUESTS = 256
N_PG = 128


def draw_adapter_of_slot(key, part):
    return (jax.random.permutation(key, 2 * ADAPTER_TOTAL) // 2).astype(jnp.int32)


def with_ends(drawn, rng, low, top_value):
    longest = drawn.shape.index(max(drawn.shape))
    spots = []
    for shift in (0, 1):
        where = [jax.random.randint(jax.random.fold_in(rng, axis), (), 0, length) for axis, length in enumerate(drawn.shape)]
        where[longest] = (where[longest] + shift) % drawn.shape[longest]
        spots.append(tuple(where))
    return drawn.at[spots[0]].set(low).at[spots[1]].set(top_value)


def steps_of(own_key, extent, shards, smallest, largest):
    level = 1.0
    for dim, blocks in shards:
        heights = jax.random.uniform(jax.random.fold_in(jax.random.fold_in(own_key, 6), dim), (blocks,), jnp.float32, smallest / len(shards), largest / len(shards))
        level = level * jnp.repeat(jnp.exp(heights), extent[dim] // blocks).reshape((-1,) + (1,) * (len(extent) - 1 - dim))
    return level


def split_up(amount, total, most, lean):
    portions = [(1 << 20) // math.isqrt(rank ** lean) + 1 for rank in range(2, amount + 1)]
    rest, holding = total - most - (amount - 1), [1] * (amount - 1)
    while rest > 0:
        movable = [i for i in range(amount - 1) if holding[i] < most]
        mass, budget = sum([portions[i] for i in movable]), rest
        for i in movable:
            more = min(most - holding[i], max(1, budget * portions[i] // mass), rest)
            holding[i] = holding[i] + more
            rest = rest - more
    return np.array([most] + holding)


def ragged(rng, amount, total, most, slope):
    if amount == 2:
        one = jax.random.randint(rng, (), max(1, total - most), min(most, total - 1) + 1)
        return jnp.stack([one, total - one])
    lengths = jnp.asarray(split_up(amount, total, most, slope), jnp.int32)
    pairs = (amount - 1) // 2
    donor, sink = lengths[1:1 + 2 * pairs:2], lengths[2:2 + 2 * pairs:2]
    slack = jnp.minimum(donor - 1, most - sink)
    shifted = jax.random.randint(jax.random.fold_in(rng, 1), (pairs,), 0, 1 << 20) % (slack + 1)
    lengths = lengths.at[1:1 + 2 * pairs:2].set(donor - shifted).at[2:2 + 2 * pairs:2].set(sink + shifted)
    return lengths[jax.random.permutation(jax.random.fold_in(rng, 2), amount)]


def shared_out(stream_key, own, number, rows, number_of, top, reach, lean):
    order = jax.random.permutation(stream_key, number_of)
    crowded, ordinary = load_shares(number_of, rows * top, reach, lean, True), load_shares(number_of, rows * top, reach, lean, False)
    places = jnp.arange(number_of)

    def named(sizes, offset_by):
        used = int((sizes > 0).sum())
        fixed = max(1, used // 4)
        moved = fixed + (places - fixed + offset_by * (used - fixed)) % max(1, number_of - fixed)
        return jnp.zeros((number_of,), jnp.int32).at[order[jnp.where(places < fixed, places, moved)]].set(jnp.asarray(sizes, jnp.int32))

    sizes = jnp.where(number % 4 == 0, named(crowded, number // 4), named(ordinary, number - number // 4 - 1))
    mixed = jax.random.permutation(jax.random.fold_in(own, 3), number_of)
    giver, receiver = mixed[0:number_of // 2 * 2:2], mixed[1:number_of // 2 * 2:2]
    margin = jnp.minimum(sizes[giver] - 1, reach - sizes[receiver]) // 2
    margin = jnp.where((giver == order[0]) | (receiver == order[0]) | (sizes[receiver] == 0), 0, jnp.maximum(margin, 0))
    moved = jax.random.randint(jax.random.fold_in(own, 4), (number_of // 2,), 0, 1 << 20) % (margin + 1)
    sizes = sizes.at[giver].add(-moved).at[receiver].add(moved)
    members = jnp.searchsorted(jnp.cumsum(sizes), jnp.arange(rows * top), side="right").astype(jnp.int32)
    listing = members.reshape(top, rows).T
    listing = listing[jax.random.permutation(jax.random.fold_in(own, 1), rows)]
    offset_by = jax.random.randint(jax.random.fold_in(own, 2), (rows, 1), 0, top)
    return jnp.take_along_axis(listing, (jnp.arange(top)[None, :] + offset_by) % top, axis=1)


def load_shares(number_of, total, bound, lean, full):
    portions = [(1 << 20) // math.isqrt(standing ** lean) + 1 for standing in range(1, number_of + 1)]
    largest = bound if full else min(bound, max(-(-total // number_of), total * portions[0] // sum(portions)))
    least = 1 if total - largest >= number_of - 1 else 0
    counts, spare = [largest] + [least] * (number_of - 1), total - largest - least * (number_of - 1)
    while spare > 0:
        free = [i for i in range(1, number_of) if counts[i] < largest] or [i for i in range(1, number_of) if counts[i] < bound]
        mass, left = sum([portions[i] for i in free]), spare
        for i in free:
            addition = min(bound - counts[i], max(1, left * portions[i] // mass), spare)
            counts[i] = counts[i] + addition
            spare = spare - addition
    return np.array(counts)


def scatter_about(rng, dims, width, reach, split=(), held_as=jnp.bfloat16):
    entries = jax.random.normal(rng, dims, jnp.float32) * width
    if len(split) > 0:
        entries = steps_of(rng, dims, split, -0.22, 0.18) * entries
    return jnp.clip(entries, min=-reach, max=reach).astype(held_as)


def setup_inputs(seed: int = 0) -> dict:
    arg_keys = jax.random.split(jax.random.key(seed), 12)
    layer_hidden_input = scatter_about(arg_keys[0], (TOKENS, MODEL_DIM), 1.0, 6.0, ((0, 128),))
    norm_scale_vector = jnp.clip(1.0 + 0.18 * jax.random.normal(arg_keys[1], (MODEL_DIM,), jnp.float32), 0.1, 1.9)
    expert_choice_index_keys = jax.random.split(jax.random.fold_in(arg_keys[2], 1), TOKENS // TOK_DEV)
    expert_choice_index_turns = jax.random.permutation(jax.random.fold_in(arg_keys[2], 3), TOKENS // TOK_DEV)
    expert_choice_index = jax.vmap(lambda own, number: shared_out(jax.random.fold_in(arg_keys[2], 2), own, number, TOK_DEV, EXPERTS, TOP, CAP, 1))(expert_choice_index_keys, expert_choice_index_turns).reshape((TOKENS, TOP))
    expert_choice_weight = jnp.clip(0.05 + 0.29999999 * jax.random.uniform(arg_keys[3], (TOKENS, TOP), jnp.float32) ** steps_of(arg_keys[3], (TOKENS, TOP), ((0, 128),), -0.2, 0.2), 0.05, 0.35)
    request_of_token = jnp.searchsorted(jnp.cumsum(ragged(arg_keys[4], REQUESTS, TOKENS, 4 * TOK_DEV, 2)), jnp.arange(TOKENS), side="right").astype(jnp.int32)
    adapter_of_request = with_ends(jax.random.randint(arg_keys[5], (REQUESTS,), 0, ADAPTER_TOTAL), jax.random.fold_in(arg_keys[5], 1), 0, ADAPTER_TOTAL - 1).astype(jnp.int32)
    adapter_of_slot = draw_adapter_of_slot(jax.random.fold_in(arg_keys[11], 71), 0)
    expert_gate_up_weight = scatter_about(arg_keys[7], (2 * EXPERTS, MODEL_DIM, 2, FF // 2), MODEL_DIM ** -0.5, 0.125, ((0, 128), (3, 2)))
    expert_down_weight = scatter_about(arg_keys[8], (2 * EXPERTS, FF // 2, MODEL_DIM), FF ** -0.5, 0.15625, ((0, 128), (1, 2)))
    adapter_down_weight = scatter_about(arg_keys[9], (2 * ADAPTER_TOTAL, MODEL_DIM, ADAPTER_RANK // 2), MODEL_DIM ** -0.5, 0.125, ((0, 128),))
    adapter_up_weight = scatter_about(arg_keys[10], (2 * ADAPTER_TOTAL, ADAPTER_RANK // 2, MODEL_DIM), (4 * ADAPTER_RANK) ** -0.5, 0.75, ((0, 128), (2, 2)))
    return {"layer_hidden_input": layer_hidden_input, "norm_scale_vector": norm_scale_vector, "expert_choice_index": expert_choice_index, "expert_choice_weight": expert_choice_weight, "request_of_token": request_of_token, "adapter_of_request": adapter_of_request, "adapter_of_slot": adapter_of_slot, "expert_gate_up_weight": expert_gate_up_weight, "expert_down_weight": expert_down_weight, "adapter_down_weight": adapter_down_weight, "adapter_up_weight": adapter_up_weight}


def normalize(states, gain_vector):
    values = states.astype(jnp.float32)
    inverse_rms = lax.rsqrt(lax.optimization_barrier(jnp.mean(values * values, axis=-1, keepdims=True)) + 1e-06)
    return (values * inverse_rms * gain_vector).astype(jnp.bfloat16)

def reference(layer_hidden_input, norm_scale_vector, expert_choice_index, expert_choice_weight, request_of_token, adapter_of_request, adapter_of_slot, expert_gate_up_weight, expert_down_weight, adapter_down_weight, adapter_up_weight):
    normalized_input = normalize(layer_hidden_input, norm_scale_vector)
    flat_ids = expert_choice_index.reshape(-1)
    weight_flat = expert_choice_weight.reshape(-1).astype(jnp.float32)
    padded_rows = jnp.concatenate([normalized_input, jnp.zeros((1, MODEL_DIM), jnp.bfloat16)], axis=0)
    padded_weights = jnp.concatenate([weight_flat, jnp.zeros((1,), jnp.float32)], axis=0)
    row_limit = N_PG * CAP
    quarter_units = FF // 4

    def one_expert(result, expert):
        positions = jnp.nonzero(flat_ids == expert, size=row_limit, fill_value=TOKENS * TOP)[0].astype(jnp.int32)
        token_index = (positions // TOP).astype(jnp.int32)
        expert_rows = padded_rows[token_index]
        contribution = jnp.zeros((row_limit, MODEL_DIM), jnp.float32)
        for half_index in range(2):
            half_slot = (2 * expert + half_index).astype(jnp.int32)
            w_in = lax.dynamic_index_in_dim(expert_gate_up_weight, half_slot, 0, keepdims=False)
            w_out = lax.dynamic_index_in_dim(expert_down_weight, half_slot, 0, keepdims=False)
            gate_up = jnp.einsum('rd,dgf->rgf', expert_rows.astype(jnp.float32), w_in.astype(jnp.float32))
            hidden = (jax.nn.silu(gate_up[:, 0]) * gate_up[:, 1]).astype(jnp.bfloat16)
            half_sum = jnp.zeros((row_limit, MODEL_DIM), jnp.float32)
            for quarter_index in range(2):
                lo_unit = quarter_index * quarter_units
                quarter = jnp.dot(hidden[:, lo_unit:lo_unit + quarter_units], w_out[lo_unit:lo_unit + quarter_units], preferred_element_type=jnp.float32)
                quarter = lax.optimization_barrier(quarter.astype(jnp.bfloat16))
                half_sum = half_sum + quarter.astype(jnp.float32)
            half_output = lax.optimization_barrier(half_sum.astype(jnp.bfloat16))
            contribution = contribution + half_output.astype(jnp.float32)
        contribution = contribution * padded_weights[positions][:, None]
        return (result.at[token_index].add(contribution), None)
    result = jnp.zeros((TOKENS + 1, MODEL_DIM), jnp.float32)
    result, _ = lax.scan(one_expert, result, jnp.arange(EXPERTS, dtype=jnp.int32))
    expert_sum = result[:TOKENS]
    token_adapter = adapter_of_request[request_of_token]
    rank_projected = jnp.einsum('ic,ycz->iyz', normalized_input.astype(jnp.float32), adapter_down_weight.astype(jnp.float32))
    matched = adapter_of_slot[None, :, None] == token_adapter[:, None, None]
    rank_projected = jnp.where(matched, rank_projected, 0.0).astype(jnp.bfloat16)
    adapter_total_output = jnp.einsum('new,ewm->nm', rank_projected.astype(jnp.float32), adapter_up_weight.astype(jnp.float32))
    return (expert_sum + adapter_total_output).astype(jnp.bfloat16)
```

```python
import jax
import jax.numpy as jnp
from jax import lax
from jax.sharding import PartitionSpec as P


def normalize(states, gain_vector):
    values = states.astype(jnp.float32)
    inverse_rms = lax.rsqrt(jnp.mean(values * values, axis=-1, keepdims=True) + 1e-06)
    return (values * inverse_rms * gain_vector).astype(jnp.bfloat16)


def expert_half(expert_rows, expert_gate_up_weight, expert_down_weight):
    gate_up = jnp.einsum(
        "rd,dgf->rgf", expert_rows, expert_gate_up_weight[0], preferred_element_type=jnp.float32
    )
    hidden = (jax.nn.silu(gate_up[:, 0]) * gate_up[:, 1]).astype(jnp.bfloat16)
    local_units = hidden.shape[1]
    piece_count = 2 // lax.axis_size("kv")
    piece_units = local_units // piece_count
    quarter = jnp.dot(
        hidden, expert_down_weight[0, 0:piece_units], preferred_element_type=jnp.float32
    )
    summed = quarter.astype(jnp.bfloat16).astype(jnp.float32)
    return lax.psum_scatter(summed.astype(jnp.bfloat16), "kv", scatter_dimension=1, tiled=True)


def rank_in_expert(flat_ids, expert_count):
    onehot = (flat_ids[:, None] == jnp.arange(expert_count, dtype=jnp.int32)[None, :]).astype(
        jnp.bfloat16
    )
    entries = flat_ids.shape[0]
    lower = (
        jnp.arange(entries, dtype=jnp.int32)[:, None]
        >= jnp.arange(entries, dtype=jnp.int32)[None, :]
    ).astype(jnp.bfloat16)
    running = jnp.dot(lower, onehot, preferred_element_type=jnp.float32)
    return (jnp.sum(running * onehot.astype(jnp.float32), axis=1) - 1.0).astype(jnp.int32)


def place_rows(slot_table, slot_total, normalized_input):
    slot_ids = jnp.arange(slot_total, dtype=jnp.int32)
    hits = jnp.zeros((slot_total, slot_table[0].shape[0]), jnp.float32)
    for table in slot_table:
        hits = hits + jnp.sum(
            (table[None, :, :] == slot_ids[:, None, None]).astype(jnp.float32), axis=2
        )
    placed = jnp.dot(
        hits.astype(jnp.bfloat16), normalized_input, preferred_element_type=jnp.float32
    )
    return placed.astype(jnp.bfloat16)


def collect_rows(slot_table, slot_total, weights, gathered):
    slot_ids = jnp.arange(slot_total, dtype=jnp.int32)
    combine = jnp.zeros((weights.shape[0], slot_total), jnp.float32)
    for table in slot_table:
        combine = combine + jnp.sum(
            jnp.where(table[:, :, None] == slot_ids[None, None, :], weights[:, :, None], 0.0),
            axis=1,
        )
    upper_part = combine.astype(jnp.bfloat16)
    lower_part = (combine - upper_part.astype(jnp.float32)).astype(jnp.bfloat16)
    return jnp.dot(upper_part, gathered, preferred_element_type=jnp.float32) + jnp.dot(
        lower_part, gathered, preferred_element_type=jnp.float32
    )


def on_device(
    layer_hidden_input,
    norm_scale_vector,
    expert_choice_index,
    expert_choice_weight,
    request_of_token,
    adapter_of_request,
    adapter_of_slot,
    expert_gate_up_weight,
    expert_down_weight,
    adapter_down_weight,
    adapter_up_weight,
):
    tok_rows, model_width = layer_hidden_input.shape
    top_count = expert_choice_index.shape[1]
    pg_size = lax.axis_size("pg")
    expert_count = pg_size // 2
    slot_cap = 4 * tok_rows * top_count // (3 * expert_count)
    half_width = model_width // lax.axis_size("kv")
    kv_index = lax.axis_index("kv")
    normalized_input = normalize(layer_hidden_input, norm_scale_vector)
    own_features = lax.dynamic_slice_in_dim(normalized_input, kv_index * half_width, half_width, axis=1)
    down_own = lax.dynamic_slice_in_dim(adapter_down_weight[0], kv_index * half_width, half_width, axis=0)
    rank_half = down_own.shape[1]
    packed = jnp.concatenate([down_own.T, adapter_up_weight[0]], axis=0)
    packed_all = lax.all_gather(packed, "pg", axis=0, tiled=False)
    flat_ids = expert_choice_index.reshape(-1)
    slot_rank = rank_in_expert(flat_ids, expert_count)
    rank_table = slot_rank.reshape(tok_rows, top_count)
    first_slot = 2 * expert_choice_index * slot_cap + rank_table
    second_slot = first_slot + slot_cap
    slot_total = pg_size * slot_cap
    outbox = place_rows((first_slot, second_slot), slot_total, own_features).reshape(
        pg_size, slot_cap, half_width
    )
    inbox_half = lax.all_to_all(outbox, "pg", split_axis=0, concat_axis=0, tiled=True)
    inbox_rows = lax.all_gather(
        inbox_half.reshape(pg_size * slot_cap, half_width), "kv", axis=1, tiled=True
    )
    half_out = expert_half(inbox_rows, expert_gate_up_weight, expert_down_weight)
    results = lax.all_to_all(
        half_out.reshape(pg_size, slot_cap, half_width),
        "pg",
        split_axis=0,
        concat_axis=0,
        tiled=True,
    )
    moe_sum = collect_rows(
        (first_slot, second_slot),
        slot_total,
        expert_choice_weight,
        results.reshape(slot_total, half_width),
    )
    request_count = adapter_of_request.shape[0]
    owner_table = request_of_token[:, None] == jnp.arange(request_count, dtype=jnp.int32)[None, :]
    token_adapter = jnp.sum(jnp.where(owner_table, adapter_of_request[None, :], 0), axis=1)
    slot_count = packed_all.shape[0]
    down_all = packed_all[:, 0:rank_half, :].reshape(slot_count * rank_half, half_width)
    up_all = packed_all[:, rank_half:, :].reshape(slot_count * rank_half, half_width)
    partial_rank = lax.dot_general(
        own_features, down_all, (((1,), (1,)), ((), ())), preferred_element_type=jnp.float32
    )
    rank_projected = lax.psum(partial_rank, "kv").reshape(tok_rows, slot_count, rank_half)
    matched = adapter_of_slot[None, :, None] == token_adapter[:, None, None]
    rank_projected = jnp.where(matched, rank_projected, 0.0).astype(jnp.bfloat16)
    flat_low = rank_projected.reshape(tok_rows, slot_count * rank_half)
    adapter_total_output = jnp.dot(flat_low, up_all, preferred_element_type=jnp.float32)
    return (moe_sum + adapter_total_output).astype(jnp.bfloat16)


def solution(mesh):
    placed = (
        P("pg", None),
        P(),
        P("pg", None),
        P("pg", None),
        P("pg"),
        P(),
        P(),
        P("pg", None, None, "kv"),
        P("pg", "kv", None),
        P("pg", None, None),
        P("pg", None, "kv"),
    )
    return jax.shard_map(
        on_device, mesh=mesh, in_specs=placed, out_specs=P("pg", "kv"), check_vma=False
    )
```

```python
import jax
import jax.numpy as jnp
from jax import lax
from jax.sharding import PartitionSpec as P


PG_AXES = ("px", "pz", "py")


def normalize(states, gain_vector):
    values = states.astype(jnp.float32)
    inverse_rms = lax.rsqrt(jnp.mean(values * values, axis=-1, keepdims=True) + 1e-06)
    return (values * inverse_rms * gain_vector).astype(jnp.bfloat16)


def expert_half(expert_rows, expert_gate_up_weight, expert_down_weight):
    gate_up = jnp.einsum(
        "rd,dgf->rgf", expert_rows, expert_gate_up_weight[0], preferred_element_type=jnp.float32
    )
    hidden = (jax.nn.silu(gate_up[:, 0]) * gate_up[:, 1]).astype(jnp.bfloat16)
    local_units = hidden.shape[1]
    piece_count = 2 // lax.axis_size("kv")
    piece_units = local_units // piece_count
    quarter = jnp.dot(
        hidden, expert_down_weight[0, 0:piece_units], preferred_element_type=jnp.float32
    )
    summed = quarter.astype(jnp.bfloat16).astype(jnp.float32)
    return lax.psum_scatter(summed.astype(jnp.bfloat16), "kv", scatter_dimension=1, tiled=True)


def rank_in_expert(flat_ids, expert_count):
    onehot = (flat_ids[:, None] == jnp.arange(expert_count, dtype=jnp.int32)[None, :]).astype(
        jnp.bfloat16
    )
    entries = flat_ids.shape[0]
    lower = (
        jnp.arange(entries, dtype=jnp.int32)[:, None]
        >= jnp.arange(entries, dtype=jnp.int32)[None, :]
    ).astype(jnp.bfloat16)
    running = jnp.dot(lower, onehot, preferred_element_type=jnp.float32)
    return (jnp.sum(running * onehot.astype(jnp.float32), axis=1) - 1.0).astype(jnp.int32)


def place_rows(slot_table, slot_total, normalized_input):
    slot_ids = jnp.arange(slot_total, dtype=jnp.int32)
    hits = jnp.zeros((slot_total, slot_table[0].shape[0]), jnp.float32)
    for table in slot_table:
        hits = hits + jnp.sum(
            (table[None, :, :] == slot_ids[:, None, None]).astype(jnp.float32), axis=2
        )
    placed = jnp.dot(
        hits.astype(jnp.bfloat16), normalized_input, preferred_element_type=jnp.float32
    )
    return placed.astype(jnp.bfloat16)


def collect_rows(slot_table, slot_total, weights, gathered):
    slot_ids = jnp.arange(slot_total, dtype=jnp.int32)
    combine = jnp.zeros((weights.shape[0], slot_total), jnp.float32)
    for table in slot_table:
        combine = combine + jnp.sum(
            jnp.where(table[:, :, None] == slot_ids[None, None, :], weights[:, :, None], 0.0),
            axis=1,
        )
    upper_part = combine.astype(jnp.bfloat16)
    lower_part = (combine - upper_part.astype(jnp.float32)).astype(jnp.bfloat16)
    return jnp.dot(upper_part, gathered, preferred_element_type=jnp.float32) + jnp.dot(
        lower_part, gathered, preferred_element_type=jnp.float32
    )


def on_device(
    layer_hidden_input,
    norm_scale_vector,
    expert_choice_index,
    expert_choice_weight,
    request_of_token,
    adapter_of_request,
    adapter_of_slot,
    expert_gate_up_weight,
    expert_down_weight,
    adapter_down_weight,
    adapter_up_weight,
):
    tok_rows, model_width = layer_hidden_input.shape
    top_count = expert_choice_index.shape[1]
    pg_size = lax.axis_size(PG_AXES)
    expert_count = pg_size // 2
    slot_cap = 4 * tok_rows * top_count // (3 * expert_count)
    half_width = model_width // lax.axis_size("kv")
    kv_index = lax.axis_index("kv")
    normalized_input = normalize(layer_hidden_input, norm_scale_vector)
    own_features = lax.dynamic_slice_in_dim(normalized_input, kv_index * half_width, half_width, axis=1)
    down_own = lax.dynamic_slice_in_dim(adapter_down_weight[0], kv_index * half_width, half_width, axis=0)
    rank_half = down_own.shape[1]
    packed = jnp.concatenate([down_own.T, adapter_up_weight[0]], axis=0)
    flat_ids = expert_choice_index.reshape(-1)
    slot_rank = rank_in_expert(flat_ids, expert_count)
    rank_table = slot_rank.reshape(tok_rows, top_count)
    first_slot = 2 * expert_choice_index * slot_cap + rank_table
    second_slot = first_slot + slot_cap
    slot_total = pg_size * slot_cap
    outbox = place_rows((first_slot, second_slot), slot_total, own_features).reshape(
        pg_size, slot_cap, half_width
    )
    inbox_half = lax.all_to_all(outbox, PG_AXES, split_axis=0, concat_axis=0, tiled=True)
    inbox_half, packed = lax.optimization_barrier((inbox_half, packed))
    packed_all = packed
    for axis_name in reversed(PG_AXES):
        packed_all = lax.all_gather(packed_all, axis_name, axis=0, tiled=False)
    packed_all = packed_all.reshape((pg_size,) + packed.shape)
    inbox_rows = lax.all_gather(
        inbox_half.reshape(pg_size * slot_cap, half_width), "kv", axis=1, tiled=True
    )
    half_out = expert_half(inbox_rows, expert_gate_up_weight, expert_down_weight)
    half_out, packed_all = lax.optimization_barrier((half_out, packed_all))
    results = lax.all_to_all(
        half_out.reshape(pg_size, slot_cap, half_width),
        PG_AXES,
        split_axis=0,
        concat_axis=0,
        tiled=True,
    )
    moe_sum = collect_rows(
        (first_slot, second_slot),
        slot_total,
        expert_choice_weight,
        results.reshape(slot_total, half_width),
    )
    request_count = adapter_of_request.shape[0]
    owner_table = request_of_token[:, None] == jnp.arange(request_count, dtype=jnp.int32)[None, :]
    token_adapter = jnp.sum(jnp.where(owner_table, adapter_of_request[None, :], 0), axis=1)
    slot_count = packed_all.shape[0]
    down_all = packed_all[:, 0:rank_half, :].reshape(slot_count * rank_half, half_width)
    up_all = packed_all[:, rank_half:, :].reshape(slot_count * rank_half, half_width)
    partial_rank = lax.dot_general(
        own_features, down_all, (((1,), (1,)), ((), ())), preferred_element_type=jnp.float32
    )
    rank_projected = lax.psum(partial_rank, "kv").reshape(tok_rows, slot_count, rank_half)
    matched = adapter_of_slot[None, :, None] == token_adapter[:, None, None]
    rank_projected = jnp.where(matched, rank_projected, 0.0).astype(jnp.bfloat16)
    flat_low = rank_projected.reshape(tok_rows, slot_count * rank_half)
    adapter_total_output = jnp.dot(flat_low, up_all, preferred_element_type=jnp.float32)
    return (moe_sum + adapter_total_output).astype(jnp.bfloat16)


def solution(mesh):
    kv_count = mesh.shape["kv"]
    pg_count = mesh.shape["pg"]
    y_count = 4 if pg_count % 4 == 0 else 1
    rest = pg_count // y_count
    z_count = 8 if rest % 8 == 0 else rest
    x_count = rest // z_count
    split_mesh = jax.sharding.Mesh(
        mesh.devices.reshape(kv_count, x_count, z_count, y_count), ("kv",) + PG_AXES
    )
    pg = PG_AXES
    placed = (
        P(pg, None),
        P(),
        P(pg, None),
        P(pg, None),
        P(pg),
        P(),
        P(),
        P(pg, None, None, "kv"),
        P(pg, "kv", None),
        P(pg, None, None),
        P(pg, None, "kv"),
    )
    return jax.shard_map(
        on_device, mesh=split_mesh, in_specs=placed, out_specs=P(pg, "kv"), check_vma=False
    )
```

```python
import jax
import jax.numpy as jnp
from jax import lax
from jax.sharding import PartitionSpec as P


PG_AXES = ("px", "pz", "py")


def normalize(states, gain_vector):
    values = states.astype(jnp.float32)
    inverse_rms = lax.rsqrt(jnp.mean(values * values, axis=-1, keepdims=True) + 1e-06)
    return (values * inverse_rms * gain_vector).astype(jnp.bfloat16)


def swap_kv(values):
    return lax.ppermute(values, "kv", perm=[(0, 1), (1, 0)])


def expert_half(own_rows, expert_gate_up_weight, expert_down_weight):
    kv_index = lax.axis_index("kv")
    half_width = own_rows.shape[1]
    other_rows = swap_kv(own_rows)
    gate_up_weight = expert_gate_up_weight[0]
    own_weight = lax.dynamic_slice_in_dim(gate_up_weight, kv_index * half_width, half_width, 0)
    other_weight = lax.dynamic_slice_in_dim(
        gate_up_weight, (1 - kv_index) * half_width, half_width, 0
    )
    gate_up = jnp.einsum(
        "rd,dgf->rgf", own_rows, own_weight, preferred_element_type=jnp.float32
    ) + jnp.einsum("rd,dgf->rgf", other_rows, other_weight, preferred_element_type=jnp.float32)
    hidden = (jax.nn.silu(gate_up[:, 0]) * gate_up[:, 1]).astype(jnp.bfloat16)
    down_weight = expert_down_weight[0]
    other_cols = lax.dynamic_slice_in_dim(down_weight, (1 - kv_index) * half_width, half_width, 1)
    own_cols = lax.dynamic_slice_in_dim(down_weight, kv_index * half_width, half_width, 1)
    sent_quarter = jnp.dot(hidden, other_cols, preferred_element_type=jnp.float32).astype(
        jnp.bfloat16
    )
    received_quarter = swap_kv(sent_quarter)
    own_quarter = jnp.dot(hidden, own_cols, preferred_element_type=jnp.float32).astype(
        jnp.bfloat16
    )
    return (own_quarter.astype(jnp.float32) + received_quarter.astype(jnp.float32)).astype(
        jnp.bfloat16
    )


def rank_in_expert(flat_ids, expert_count):
    onehot = (flat_ids[:, None] == jnp.arange(expert_count, dtype=jnp.int32)[None, :]).astype(
        jnp.bfloat16
    )
    entries = flat_ids.shape[0]
    lower = (
        jnp.arange(entries, dtype=jnp.int32)[:, None]
        >= jnp.arange(entries, dtype=jnp.int32)[None, :]
    ).astype(jnp.bfloat16)
    running = jnp.dot(lower, onehot, preferred_element_type=jnp.float32)
    return (jnp.sum(running * onehot.astype(jnp.float32), axis=1) - 1.0).astype(jnp.int32)


def place_rows(slot_table, slot_total, normalized_input):
    slot_ids = jnp.arange(slot_total, dtype=jnp.int32)
    hits = jnp.zeros((slot_total, slot_table[0].shape[0]), jnp.float32)
    for table in slot_table:
        hits = hits + jnp.sum(
            (table[None, :, :] == slot_ids[:, None, None]).astype(jnp.float32), axis=2
        )
    placed = jnp.dot(
        hits.astype(jnp.bfloat16), normalized_input, preferred_element_type=jnp.float32
    )
    return placed.astype(jnp.bfloat16)


def collect_rows(slot_table, slot_total, weights, gathered):
    slot_ids = jnp.arange(slot_total, dtype=jnp.int32)
    combine = jnp.zeros((weights.shape[0], slot_total), jnp.float32)
    for table in slot_table:
        combine = combine + jnp.sum(
            jnp.where(table[:, :, None] == slot_ids[None, None, :], weights[:, :, None], 0.0),
            axis=1,
        )
    upper_part = combine.astype(jnp.bfloat16)
    lower_part = (combine - upper_part.astype(jnp.float32)).astype(jnp.bfloat16)
    return jnp.dot(upper_part, gathered, preferred_element_type=jnp.float32) + jnp.dot(
        lower_part, gathered, preferred_element_type=jnp.float32
    )


def on_device(
    layer_hidden_input,
    norm_scale_vector,
    expert_choice_index,
    expert_choice_weight,
    request_of_token,
    adapter_of_request,
    adapter_of_slot,
    expert_gate_up_weight,
    expert_down_weight,
    adapter_down_weight,
    adapter_up_weight,
):
    tok_rows, model_width = layer_hidden_input.shape
    top_count = expert_choice_index.shape[1]
    pg_size = lax.axis_size(PG_AXES)
    expert_count = pg_size // 2
    slot_cap = 4 * tok_rows * top_count // (3 * expert_count)
    half_width = model_width // lax.axis_size("kv")
    kv_index = lax.axis_index("kv")
    normalized_input = normalize(layer_hidden_input, norm_scale_vector)
    own_features = lax.dynamic_slice_in_dim(normalized_input, kv_index * half_width, half_width, axis=1)
    down_own = lax.dynamic_slice_in_dim(adapter_down_weight[0], kv_index * half_width, half_width, axis=0)
    rank_half = down_own.shape[1]
    packed = jnp.concatenate([down_own.T, adapter_up_weight[0]], axis=0)
    flat_ids = expert_choice_index.reshape(-1)
    slot_rank = rank_in_expert(flat_ids, expert_count)
    rank_table = slot_rank.reshape(tok_rows, top_count)
    first_slot = 2 * expert_choice_index * slot_cap + rank_table
    second_slot = first_slot + slot_cap
    slot_total = pg_size * slot_cap
    outbox = place_rows((first_slot, second_slot), slot_total, own_features).reshape(
        pg_size, slot_cap, half_width
    )
    outbox, packed = lax.optimization_barrier((outbox, packed))
    inbox_half = lax.all_to_all(outbox, PG_AXES, split_axis=0, concat_axis=0, tiled=True)
    packed_all = packed
    for axis_name in reversed(PG_AXES):
        packed_all = lax.all_gather(packed_all, axis_name, axis=0, tiled=False)
    packed_all = packed_all.reshape((pg_size,) + packed.shape)
    half_out = expert_half(inbox_half.reshape(pg_size * slot_cap, half_width), expert_gate_up_weight, expert_down_weight)
    half_out, packed_all = lax.optimization_barrier((half_out, packed_all))
    results = lax.all_to_all(
        half_out.reshape(pg_size, slot_cap, half_width),
        PG_AXES,
        split_axis=0,
        concat_axis=0,
        tiled=True,
    )
    moe_sum = collect_rows(
        (first_slot, second_slot),
        slot_total,
        expert_choice_weight,
        results.reshape(slot_total, half_width),
    )
    request_count = adapter_of_request.shape[0]
    owner_table = request_of_token[:, None] == jnp.arange(request_count, dtype=jnp.int32)[None, :]
    token_adapter = jnp.sum(jnp.where(owner_table, adapter_of_request[None, :], 0), axis=1)
    slot_count = packed_all.shape[0]
    down_all = packed_all[:, 0:rank_half, :].reshape(slot_count * rank_half, half_width)
    up_all = packed_all[:, rank_half:, :].reshape(slot_count * rank_half, half_width)
    partial_rank = lax.dot_general(
        own_features, down_all, (((1,), (1,)), ((), ())), preferred_element_type=jnp.float32
    )
    rank_projected = lax.psum(partial_rank, "kv").reshape(tok_rows, slot_count, rank_half)
    matched = adapter_of_slot[None, :, None] == token_adapter[:, None, None]
    rank_projected = jnp.where(matched, rank_projected, 0.0).astype(jnp.bfloat16)
    flat_low = rank_projected.reshape(tok_rows, slot_count * rank_half)
    adapter_total_output = jnp.dot(flat_low, up_all, preferred_element_type=jnp.float32)
    return (moe_sum + adapter_total_output).astype(jnp.bfloat16)


def solution(mesh):
    kv_count = mesh.shape["kv"]
    pg_count = mesh.shape["pg"]
    y_count = 4 if pg_count % 4 == 0 else 1
    rest = pg_count // y_count
    z_count = 8 if rest % 8 == 0 else rest
    x_count = rest // z_count
    split_mesh = jax.sharding.Mesh(
        mesh.devices.reshape(kv_count, x_count, z_count, y_count), ("kv",) + PG_AXES
    )
    pg = PG_AXES
    placed = (
        P(pg, None),
        P(),
        P(pg, None),
        P(pg, None),
        P(pg),
        P(),
        P(),
        P(pg, None, None, "kv"),
        P(pg, "kv", None),
        P(pg, None, None),
        P(pg, None, "kv"),
    )
    return jax.shard_map(
        on_device, mesh=split_mesh, in_specs=placed, out_specs=P(pg, "kv"), check_vma=False
    )
```

```python
import jax
import jax.numpy as jnp
from jax import lax
from jax.sharding import PartitionSpec as P


PG_AXES = ("px", "pz", "py")


def normalize(states, gain_vector):
    values = states.astype(jnp.float32)
    inverse_rms = lax.rsqrt(jnp.mean(values * values, axis=-1, keepdims=True) + 1e-06)
    return (values * inverse_rms * gain_vector).astype(jnp.bfloat16)


def swap_kv(values):
    return lax.ppermute(values, "kv", perm=[(0, 1), (1, 0)])


def expert_half(own_rows, expert_gate_up_weight, expert_down_weight):
    kv_index = lax.axis_index("kv")
    half_width = own_rows.shape[1]
    other_rows = swap_kv(own_rows)
    gate_up_weight = expert_gate_up_weight[0]
    own_weight = lax.dynamic_slice_in_dim(gate_up_weight, kv_index * half_width, half_width, 0)
    other_weight = lax.dynamic_slice_in_dim(
        gate_up_weight, (1 - kv_index) * half_width, half_width, 0
    )
    gate_up = jnp.einsum(
        "rd,dgf->rgf", own_rows, own_weight, preferred_element_type=jnp.float32
    ) + jnp.einsum("rd,dgf->rgf", other_rows, other_weight, preferred_element_type=jnp.float32)
    hidden = (jax.nn.silu(gate_up[:, 0]) * gate_up[:, 1]).astype(jnp.bfloat16)
    down_weight = expert_down_weight[0]
    other_cols = lax.dynamic_slice_in_dim(down_weight, (1 - kv_index) * half_width, half_width, 1)
    own_cols = lax.dynamic_slice_in_dim(down_weight, kv_index * half_width, half_width, 1)
    sent_quarter = jnp.dot(hidden, other_cols, preferred_element_type=jnp.float32).astype(
        jnp.bfloat16
    )
    received_quarter = swap_kv(sent_quarter)
    own_quarter = jnp.dot(hidden, own_cols, preferred_element_type=jnp.float32).astype(
        jnp.bfloat16
    )
    return (own_quarter.astype(jnp.float32) + received_quarter.astype(jnp.float32)).astype(
        jnp.bfloat16
    )


def rank_in_expert(flat_ids, expert_count):
    onehot = (flat_ids[:, None] == jnp.arange(expert_count, dtype=jnp.int32)[None, :]).astype(
        jnp.bfloat16
    )
    entries = flat_ids.shape[0]
    lower = (
        jnp.arange(entries, dtype=jnp.int32)[:, None]
        >= jnp.arange(entries, dtype=jnp.int32)[None, :]
    ).astype(jnp.bfloat16)
    running = jnp.dot(lower, onehot, preferred_element_type=jnp.float32)
    return (jnp.sum(running * onehot.astype(jnp.float32), axis=1) - 1.0).astype(jnp.int32)


def place_rows(slot_table, slot_total, normalized_input):
    slot_ids = jnp.arange(slot_total, dtype=jnp.int32)
    hits = jnp.zeros((slot_total, slot_table[0].shape[0]), jnp.float32)
    for table in slot_table:
        hits = hits + jnp.sum(
            (table[None, :, :] == slot_ids[:, None, None]).astype(jnp.float32), axis=2
        )
    placed = jnp.dot(
        hits.astype(jnp.bfloat16), normalized_input, preferred_element_type=jnp.float32
    )
    return placed.astype(jnp.bfloat16)


def collect_rows(slot_table, slot_total, weights, gathered):
    slot_ids = jnp.arange(slot_total, dtype=jnp.int32)
    combine = jnp.zeros((weights.shape[0], slot_total), jnp.float32)
    for table in slot_table:
        combine = combine + jnp.sum(
            jnp.where(table[:, :, None] == slot_ids[None, None, :], weights[:, :, None], 0.0),
            axis=1,
        )
    upper_part = combine.astype(jnp.bfloat16)
    lower_part = (combine - upper_part.astype(jnp.float32)).astype(jnp.bfloat16)
    return jnp.dot(upper_part, gathered, preferred_element_type=jnp.float32) + jnp.dot(
        lower_part, gathered, preferred_element_type=jnp.float32
    )


def on_device(
    layer_hidden_input,
    norm_scale_vector,
    expert_choice_index,
    expert_choice_weight,
    request_of_token,
    adapter_of_request,
    adapter_of_slot,
    expert_gate_up_weight,
    expert_down_weight,
    adapter_down_weight,
    adapter_up_weight,
):
    tok_rows, model_width = layer_hidden_input.shape
    top_count = expert_choice_index.shape[1]
    pg_size = lax.axis_size(PG_AXES)
    expert_count = pg_size // 2
    slot_cap = 4 * tok_rows * top_count // (3 * expert_count)
    half_width = model_width // lax.axis_size("kv")
    kv_index = lax.axis_index("kv")
    normalized_input = normalize(layer_hidden_input, norm_scale_vector)
    own_features = lax.dynamic_slice_in_dim(normalized_input, kv_index * half_width, half_width, axis=1)
    down_own = lax.dynamic_slice_in_dim(adapter_down_weight[0], kv_index * half_width, half_width, axis=0)
    rank_half = down_own.shape[1]
    packed = jnp.concatenate([down_own.T, adapter_up_weight[0]], axis=0)
    flat_ids = expert_choice_index.reshape(-1)
    slot_rank = rank_in_expert(flat_ids, expert_count)
    rank_table = slot_rank.reshape(tok_rows, top_count)
    first_slot = 2 * expert_choice_index * slot_cap + rank_table
    second_slot = first_slot + slot_cap
    slot_total = pg_size * slot_cap
    outbox = place_rows((first_slot, second_slot), slot_total, own_features).reshape(
        pg_size, slot_cap, half_width
    )
    inbox_half = lax.all_to_all(outbox, PG_AXES, split_axis=0, concat_axis=0, tiled=True)
    packed_all = lax.all_gather(packed, PG_AXES, axis=0, tiled=False)
    half_out = expert_half(inbox_half.reshape(pg_size * slot_cap, half_width), expert_gate_up_weight, expert_down_weight)
    results = lax.all_to_all(
        half_out.reshape(pg_size, slot_cap, half_width),
        PG_AXES,
        split_axis=0,
        concat_axis=0,
        tiled=True,
    )
    moe_sum = collect_rows(
        (first_slot, second_slot),
        slot_total,
        expert_choice_weight,
        results.reshape(slot_total, half_width),
    )
    request_count = adapter_of_request.shape[0]
    owner_table = request_of_token[:, None] == jnp.arange(request_count, dtype=jnp.int32)[None, :]
    token_adapter = jnp.sum(jnp.where(owner_table, adapter_of_request[None, :], 0), axis=1)
    slot_count = packed_all.shape[0]
    down_all = packed_all[:, 0:rank_half, :].reshape(slot_count * rank_half, half_width)
    up_all = packed_all[:, rank_half:, :].reshape(slot_count * rank_half, half_width)
    partial_rank = lax.dot_general(
        own_features, down_all, (((1,), (1,)), ((), ())), preferred_element_type=jnp.float32
    )
    rank_projected = lax.psum(partial_rank, "kv").reshape(tok_rows, slot_count, rank_half)
    matched = adapter_of_slot[None, :, None] == token_adapter[:, None, None]
    rank_projected = jnp.where(matched, rank_projected, 0.0).astype(jnp.bfloat16)
    flat_low = rank_projected.reshape(tok_rows, slot_count * rank_half)
    adapter_total_output = jnp.dot(flat_low, up_all, preferred_element_type=jnp.float32)
    return (moe_sum + adapter_total_output).astype(jnp.bfloat16)


def solution(mesh):
    kv_count = mesh.shape["kv"]
    pg_count = mesh.shape["pg"]
    y_count = 4 if pg_count % 4 == 0 else 1
    rest = pg_count // y_count
    z_count = 8 if rest % 8 == 0 else rest
    x_count = rest // z_count
    split_mesh = jax.sharding.Mesh(
        mesh.devices.reshape(kv_count, x_count, z_count, y_count), ("kv",) + PG_AXES
    )
    pg = PG_AXES
    placed = (
        P(pg, None),
        P(),
        P(pg, None),
        P(pg, None),
        P(pg),
        P(),
        P(),
        P(pg, None, None, "kv"),
        P(pg, "kv", None),
        P(pg, None, None),
        P(pg, None, "kv"),
    )
    return jax.shard_map(
        on_device, mesh=split_mesh, in_specs=placed, out_specs=P(pg, "kv"), check_vma=False
    )
```

```python
import jax
import jax.numpy as jnp
from jax import lax
from jax.sharding import PartitionSpec as P


PG_AXES = ("px", "pz", "py")


def normalize(states, gain_vector):
    values = states.astype(jnp.float32)
    inverse_rms = lax.rsqrt(jnp.mean(values * values, axis=-1, keepdims=True) + 1e-06)
    return (values * inverse_rms * gain_vector).astype(jnp.bfloat16)


def swap_kv(values):
    return lax.ppermute(values, "kv", perm=[(0, 1), (1, 0)])


def expert_half(own_rows, expert_gate_up_weight, expert_down_weight):
    kv_index = lax.axis_index("kv")
    half_width = own_rows.shape[1]
    other_rows = swap_kv(own_rows)
    gate_up_weight = expert_gate_up_weight[0]
    own_weight = lax.dynamic_slice_in_dim(gate_up_weight, kv_index * half_width, half_width, 0)
    other_weight = lax.dynamic_slice_in_dim(
        gate_up_weight, (1 - kv_index) * half_width, half_width, 0
    )
    gate_up = jnp.einsum(
        "rd,dgf->rgf", own_rows, own_weight, preferred_element_type=jnp.float32
    ) + jnp.einsum("rd,dgf->rgf", other_rows, other_weight, preferred_element_type=jnp.float32)
    hidden = (jax.nn.silu(gate_up[:, 0]) * gate_up[:, 1]).astype(jnp.bfloat16)
    down_weight = expert_down_weight[0]
    other_cols = lax.dynamic_slice_in_dim(down_weight, (1 - kv_index) * half_width, half_width, 1)
    own_cols = lax.dynamic_slice_in_dim(down_weight, kv_index * half_width, half_width, 1)
    sent_quarter = jnp.dot(hidden, other_cols, preferred_element_type=jnp.float32).astype(
        jnp.bfloat16
    )
    received_quarter = swap_kv(sent_quarter)
    own_quarter = jnp.dot(hidden, own_cols, preferred_element_type=jnp.float32).astype(
        jnp.bfloat16
    )
    return (own_quarter.astype(jnp.float32) + received_quarter.astype(jnp.float32)).astype(
        jnp.bfloat16
    )


def rank_in_expert(flat_ids, expert_count):
    onehot = (flat_ids[:, None] == jnp.arange(expert_count, dtype=jnp.int32)[None, :]).astype(
        jnp.bfloat16
    )
    entries = flat_ids.shape[0]
    lower = (
        jnp.arange(entries, dtype=jnp.int32)[:, None]
        >= jnp.arange(entries, dtype=jnp.int32)[None, :]
    ).astype(jnp.bfloat16)
    running = jnp.dot(lower, onehot, preferred_element_type=jnp.float32)
    return (jnp.sum(running * onehot.astype(jnp.float32), axis=1) - 1.0).astype(jnp.int32)


def place_rows(slot_table, slot_total, normalized_input):
    slot_ids = jnp.arange(slot_total, dtype=jnp.int32)
    hits = jnp.zeros((slot_total, slot_table[0].shape[0]), jnp.float32)
    for table in slot_table:
        hits = hits + jnp.sum(
            (table[None, :, :] == slot_ids[:, None, None]).astype(jnp.float32), axis=2
        )
    placed = jnp.dot(
        hits.astype(jnp.bfloat16), normalized_input, preferred_element_type=jnp.float32
    )
    return placed.astype(jnp.bfloat16)


def collect_rows(slot_table, slot_total, weights, gathered):
    slot_ids = jnp.arange(slot_total, dtype=jnp.int32)
    combine = jnp.zeros((weights.shape[0], slot_total), jnp.float32)
    for table in slot_table:
        combine = combine + jnp.sum(
            jnp.where(table[:, :, None] == slot_ids[None, None, :], weights[:, :, None], 0.0),
            axis=1,
        )
    upper_part = combine.astype(jnp.bfloat16)
    lower_part = (combine - upper_part.astype(jnp.float32)).astype(jnp.bfloat16)
    return jnp.dot(upper_part, gathered, preferred_element_type=jnp.float32) + jnp.dot(
        lower_part, gathered, preferred_element_type=jnp.float32
    )


def on_device(
    layer_hidden_input,
    norm_scale_vector,
    expert_choice_index,
    expert_choice_weight,
    request_of_token,
    adapter_of_request,
    adapter_of_slot,
    expert_gate_up_weight,
    expert_down_weight,
    adapter_down_weight,
    adapter_up_weight,
):
    tok_rows, model_width = layer_hidden_input.shape
    top_count = expert_choice_index.shape[1]
    pg_size = lax.axis_size(PG_AXES)
    expert_count = pg_size // 2
    slot_cap = 4 * tok_rows * top_count // (3 * expert_count)
    half_width = model_width // lax.axis_size("kv")
    kv_index = lax.axis_index("kv")
    normalized_input = normalize(layer_hidden_input, norm_scale_vector)
    own_features = lax.dynamic_slice_in_dim(normalized_input, kv_index * half_width, half_width, axis=1)
    down_own = lax.dynamic_slice_in_dim(adapter_down_weight[0], kv_index * half_width, half_width, axis=0)
    rank_half = down_own.shape[1]
    packed = jnp.concatenate([down_own.T, adapter_up_weight[0]], axis=0)
    flat_ids = expert_choice_index.reshape(-1)
    slot_rank = rank_in_expert(flat_ids, expert_count)
    rank_table = slot_rank.reshape(tok_rows, top_count)
    first_slot = 2 * expert_choice_index * slot_cap + rank_table
    second_slot = first_slot + slot_cap
    slot_total = pg_size * slot_cap
    outbox = place_rows((first_slot, second_slot), slot_total, own_features).reshape(
        pg_size, slot_cap, half_width
    )
    inbox_half = lax.all_to_all(outbox, PG_AXES, split_axis=0, concat_axis=0, tiled=True)
    packed_all = lax.all_gather(packed, PG_AXES, axis=0, tiled=False)
    inbox_half, packed_all = lax.optimization_barrier((inbox_half, packed_all))
    half_out = expert_half(inbox_half.reshape(pg_size * slot_cap, half_width), expert_gate_up_weight, expert_down_weight)
    results = lax.all_to_all(
        half_out.reshape(pg_size, slot_cap, half_width),
        PG_AXES,
        split_axis=0,
        concat_axis=0,
        tiled=True,
    )
    moe_sum = collect_rows(
        (first_slot, second_slot),
        slot_total,
        expert_choice_weight,
        results.reshape(slot_total, half_width),
    )
    request_count = adapter_of_request.shape[0]
    owner_table = request_of_token[:, None] == jnp.arange(request_count, dtype=jnp.int32)[None, :]
    token_adapter = jnp.sum(jnp.where(owner_table, adapter_of_request[None, :], 0), axis=1)
    slot_count = packed_all.shape[0]
    down_all = packed_all[:, 0:rank_half, :].reshape(slot_count * rank_half, half_width)
    up_all = packed_all[:, rank_half:, :].reshape(slot_count * rank_half, half_width)
    partial_rank = lax.dot_general(
        own_features, down_all, (((1,), (1,)), ((), ())), preferred_element_type=jnp.float32
    )
    rank_projected = lax.psum(partial_rank, "kv").reshape(tok_rows, slot_count, rank_half)
    matched = adapter_of_slot[None, :, None] == token_adapter[:, None, None]
    rank_projected = jnp.where(matched, rank_projected, 0.0).astype(jnp.bfloat16)
    flat_low = rank_projected.reshape(tok_rows, slot_count * rank_half)
    adapter_total_output = jnp.dot(flat_low, up_all, preferred_element_type=jnp.float32)
    return (moe_sum + adapter_total_output).astype(jnp.bfloat16)


def solution(mesh):
    kv_count = mesh.shape["kv"]
    pg_count = mesh.shape["pg"]
    y_count = 4 if pg_count % 4 == 0 else 1
    rest = pg_count // y_count
    z_count = 8 if rest % 8 == 0 else rest
    x_count = rest // z_count
    split_mesh = jax.sharding.Mesh(
        mesh.devices.reshape(kv_count, x_count, z_count, y_count), ("kv",) + PG_AXES
    )
    pg = PG_AXES
    placed = (
        P(pg, None),
        P(),
        P(pg, None),
        P(pg, None),
        P(pg),
        P(),
        P(),
        P(pg, None, None, "kv"),
        P(pg, "kv", None),
        P(pg, None, None),
        P(pg, None, "kv"),
    )
    return jax.shard_map(
        on_device, mesh=split_mesh, in_specs=placed, out_specs=P(pg, "kv"), check_vma=False
    )
```

```python
import jax
import jax.numpy as jnp
from jax import lax
from jax.sharding import PartitionSpec as P


PG_AXES = ("px", "pz", "py")


def normalize(states, gain_vector):
    values = states.astype(jnp.float32)
    inverse_rms = lax.rsqrt(jnp.mean(values * values, axis=-1, keepdims=True) + 1e-06)
    return (values * inverse_rms * gain_vector).astype(jnp.bfloat16)


def shift_gather(block, axis_name):
    count = lax.axis_size(axis_name)
    pieces = [block]
    for shift in range(1, count):
        pieces.append(
            lax.ppermute(
                block, axis_name, perm=[(j, (j + shift) % count) for j in range(count)]
            )
        )
    return jnp.stack(pieces)


def gathered_slot_order(axis_order):
    sizes = {name: lax.axis_size(name) for name in PG_AXES}
    grids = jnp.meshgrid(
        *[jnp.arange(sizes[name], dtype=jnp.int32) for name in reversed(axis_order)],
        indexing="ij",
    )
    source = {}
    for name, offsets in zip(reversed(axis_order), grids):
        own = lax.axis_index(name).astype(jnp.int32)
        source[name] = (own - offsets) % sizes[name]
    slot = jnp.zeros_like(grids[0])
    for name in PG_AXES:
        slot = slot * sizes[name] + source[name]
    return slot.reshape(-1)


def swap_kv(values):
    return lax.ppermute(values, "kv", perm=[(0, 1), (1, 0)])


def expert_half(own_rows, expert_gate_up_weight, expert_down_weight):
    kv_index = lax.axis_index("kv")
    half_width = own_rows.shape[1]
    other_rows = swap_kv(own_rows)
    gate_up_weight = expert_gate_up_weight[0]
    own_weight = lax.dynamic_slice_in_dim(gate_up_weight, kv_index * half_width, half_width, 0)
    other_weight = lax.dynamic_slice_in_dim(
        gate_up_weight, (1 - kv_index) * half_width, half_width, 0
    )
    gate_up = jnp.einsum(
        "rd,dgf->rgf", own_rows, own_weight, preferred_element_type=jnp.float32
    ) + jnp.einsum("rd,dgf->rgf", other_rows, other_weight, preferred_element_type=jnp.float32)
    hidden = (jax.nn.silu(gate_up[:, 0]) * gate_up[:, 1]).astype(jnp.bfloat16)
    down_weight = expert_down_weight[0]
    other_cols = lax.dynamic_slice_in_dim(down_weight, (1 - kv_index) * half_width, half_width, 1)
    own_cols = lax.dynamic_slice_in_dim(down_weight, kv_index * half_width, half_width, 1)
    sent_quarter = jnp.dot(hidden, other_cols, preferred_element_type=jnp.float32).astype(
        jnp.bfloat16
    )
    received_quarter = swap_kv(sent_quarter)
    own_quarter = jnp.dot(hidden, own_cols, preferred_element_type=jnp.float32).astype(
        jnp.bfloat16
    )
    return (own_quarter.astype(jnp.float32) + received_quarter.astype(jnp.float32)).astype(
        jnp.bfloat16
    )


def rank_in_expert(flat_ids, expert_count):
    onehot = (flat_ids[:, None] == jnp.arange(expert_count, dtype=jnp.int32)[None, :]).astype(
        jnp.bfloat16
    )
    entries = flat_ids.shape[0]
    lower = (
        jnp.arange(entries, dtype=jnp.int32)[:, None]
        >= jnp.arange(entries, dtype=jnp.int32)[None, :]
    ).astype(jnp.bfloat16)
    running = jnp.dot(lower, onehot, preferred_element_type=jnp.float32)
    return (jnp.sum(running * onehot.astype(jnp.float32), axis=1) - 1.0).astype(jnp.int32)


def place_rows(slot_table, slot_total, normalized_input):
    slot_ids = jnp.arange(slot_total, dtype=jnp.int32)
    hits = jnp.zeros((slot_total, slot_table[0].shape[0]), jnp.float32)
    for table in slot_table:
        hits = hits + jnp.sum(
            (table[None, :, :] == slot_ids[:, None, None]).astype(jnp.float32), axis=2
        )
    placed = jnp.dot(
        hits.astype(jnp.bfloat16), normalized_input, preferred_element_type=jnp.float32
    )
    return placed.astype(jnp.bfloat16)


def collect_rows(slot_table, slot_total, weights, gathered):
    slot_ids = jnp.arange(slot_total, dtype=jnp.int32)
    combine = jnp.zeros((weights.shape[0], slot_total), jnp.float32)
    for table in slot_table:
        combine = combine + jnp.sum(
            jnp.where(table[:, :, None] == slot_ids[None, None, :], weights[:, :, None], 0.0),
            axis=1,
        )
    upper_part = combine.astype(jnp.bfloat16)
    lower_part = (combine - upper_part.astype(jnp.float32)).astype(jnp.bfloat16)
    return jnp.dot(upper_part, gathered, preferred_element_type=jnp.float32) + jnp.dot(
        lower_part, gathered, preferred_element_type=jnp.float32
    )


def on_device(
    layer_hidden_input,
    norm_scale_vector,
    expert_choice_index,
    expert_choice_weight,
    request_of_token,
    adapter_of_request,
    adapter_of_slot,
    expert_gate_up_weight,
    expert_down_weight,
    adapter_down_weight,
    adapter_up_weight,
):
    tok_rows, model_width = layer_hidden_input.shape
    top_count = expert_choice_index.shape[1]
    pg_size = lax.axis_size(PG_AXES)
    expert_count = pg_size // 2
    slot_cap = 4 * tok_rows * top_count // (3 * expert_count)
    half_width = model_width // lax.axis_size("kv")
    kv_index = lax.axis_index("kv")
    normalized_input = normalize(layer_hidden_input, norm_scale_vector)
    own_features = lax.dynamic_slice_in_dim(normalized_input, kv_index * half_width, half_width, axis=1)
    down_own = lax.dynamic_slice_in_dim(adapter_down_weight[0], kv_index * half_width, half_width, axis=0)
    rank_half = down_own.shape[1]
    packed = jnp.concatenate([down_own.T, adapter_up_weight[0]], axis=0)
    flat_ids = expert_choice_index.reshape(-1)
    slot_rank = rank_in_expert(flat_ids, expert_count)
    rank_table = slot_rank.reshape(tok_rows, top_count)
    first_slot = 2 * expert_choice_index * slot_cap + rank_table
    second_slot = first_slot + slot_cap
    slot_total = pg_size * slot_cap
    outbox = place_rows((first_slot, second_slot), slot_total, own_features).reshape(
        pg_size, slot_cap, half_width
    )
    inbox_half = lax.all_to_all(outbox, PG_AXES, split_axis=0, concat_axis=0, tiled=True)
    gather_order = ("pz", "py", "px")
    packed_all = packed
    for axis_name in gather_order:
        packed_all = shift_gather(packed_all, axis_name)
    packed_all = packed_all.reshape((pg_size,) + packed.shape)
    adapter_of_position = adapter_of_slot[gathered_slot_order(gather_order)]
    inbox_half, packed_all = lax.optimization_barrier((inbox_half, packed_all))
    half_out = expert_half(inbox_half.reshape(pg_size * slot_cap, half_width), expert_gate_up_weight, expert_down_weight)
    results = lax.all_to_all(
        half_out.reshape(pg_size, slot_cap, half_width),
        PG_AXES,
        split_axis=0,
        concat_axis=0,
        tiled=True,
    )
    moe_sum = collect_rows(
        (first_slot, second_slot),
        slot_total,
        expert_choice_weight,
        results.reshape(slot_total, half_width),
    )
    request_count = adapter_of_request.shape[0]
    owner_table = request_of_token[:, None] == jnp.arange(request_count, dtype=jnp.int32)[None, :]
    token_adapter = jnp.sum(jnp.where(owner_table, adapter_of_request[None, :], 0), axis=1)
    slot_count = packed_all.shape[0]
    down_all = packed_all[:, 0:rank_half, :].reshape(slot_count * rank_half, half_width)
    up_all = packed_all[:, rank_half:, :].reshape(slot_count * rank_half, half_width)
    partial_rank = lax.dot_general(
        own_features, down_all, (((1,), (1,)), ((), ())), preferred_element_type=jnp.float32
    )
    rank_projected = lax.psum(partial_rank, "kv").reshape(tok_rows, slot_count, rank_half)
    matched = adapter_of_position[None, :, None] == token_adapter[:, None, None]
    rank_projected = jnp.where(matched, rank_projected, 0.0).astype(jnp.bfloat16)
    flat_low = rank_projected.reshape(tok_rows, slot_count * rank_half)
    adapter_total_output = jnp.dot(flat_low, up_all, preferred_element_type=jnp.float32)
    return (moe_sum + adapter_total_output).astype(jnp.bfloat16)


def solution(mesh):
    kv_count = mesh.shape["kv"]
    pg_count = mesh.shape["pg"]
    y_count = 4 if pg_count % 4 == 0 else 1
    rest = pg_count // y_count
    z_count = 8 if rest % 8 == 0 else rest
    x_count = rest // z_count
    split_mesh = jax.sharding.Mesh(
        mesh.devices.reshape(kv_count, x_count, z_count, y_count), ("kv",) + PG_AXES
    )
    pg = PG_AXES
    placed = (
        P(pg, None),
        P(),
        P(pg, None),
        P(pg, None),
        P(pg),
        P(),
        P(),
        P(pg, None, None, "kv"),
        P(pg, "kv", None),
        P(pg, None, None),
        P(pg, None, "kv"),
    )
    return jax.shard_map(
        on_device, mesh=split_mesh, in_specs=placed, out_specs=P(pg, "kv"), check_vma=False
    )
```

```python
import jax
import jax.numpy as jnp
from jax import lax
from jax.sharding import PartitionSpec as P


PG_AXES = ("px", "pz", "py")


def normalize(states, gain_vector):
    values = states.astype(jnp.float32)
    inverse_rms = lax.rsqrt(jnp.mean(values * values, axis=-1, keepdims=True) + 1e-06)
    return (values * inverse_rms * gain_vector).astype(jnp.bfloat16)


def swap_kv(values):
    return lax.ppermute(values, "kv", perm=[(0, 1), (1, 0)])


def expert_half(own_rows, weights):
    own_weight, other_weight, own_cols, other_cols = weights
    other_rows = swap_kv(own_rows)
    gate_up = jnp.einsum(
        "rd,dgf->rgf", own_rows, own_weight, preferred_element_type=jnp.float32
    ) + jnp.einsum("rd,dgf->rgf", other_rows, other_weight, preferred_element_type=jnp.float32)
    hidden = (jax.nn.silu(gate_up[:, 0]) * gate_up[:, 1]).astype(jnp.bfloat16)
    sent_quarter = jnp.dot(hidden, other_cols, preferred_element_type=jnp.float32).astype(
        jnp.bfloat16
    )
    received_quarter = swap_kv(sent_quarter)
    own_quarter = jnp.dot(hidden, own_cols, preferred_element_type=jnp.float32).astype(
        jnp.bfloat16
    )
    own_quarter, received_quarter = lax.optimization_barrier((own_quarter, received_quarter))
    return (own_quarter.astype(jnp.float32) + received_quarter.astype(jnp.float32)).astype(
        jnp.bfloat16
    )


def split_weights(expert_gate_up_weight, expert_down_weight, half_width):
    kv_index = lax.axis_index("kv")
    gate_up_weight = expert_gate_up_weight[0]
    own_weight = lax.dynamic_slice_in_dim(gate_up_weight, kv_index * half_width, half_width, 0)
    other_weight = lax.dynamic_slice_in_dim(
        gate_up_weight, (1 - kv_index) * half_width, half_width, 0
    )
    down_weight = expert_down_weight[0]
    own_cols = lax.dynamic_slice_in_dim(down_weight, kv_index * half_width, half_width, 1)
    other_cols = lax.dynamic_slice_in_dim(down_weight, (1 - kv_index) * half_width, half_width, 1)
    return own_weight, other_weight, own_cols, other_cols


def rank_in_expert(flat_ids, expert_count):
    onehot = (flat_ids[:, None] == jnp.arange(expert_count, dtype=jnp.int32)[None, :]).astype(
        jnp.bfloat16
    )
    entries = flat_ids.shape[0]
    lower = (
        jnp.arange(entries, dtype=jnp.int32)[:, None]
        >= jnp.arange(entries, dtype=jnp.int32)[None, :]
    ).astype(jnp.bfloat16)
    running = jnp.dot(lower, onehot, preferred_element_type=jnp.float32)
    return (jnp.sum(running * onehot.astype(jnp.float32), axis=1) - 1.0).astype(jnp.int32)


def place_rows(slot_table, slot_total, normalized_input):
    slot_ids = jnp.arange(slot_total, dtype=jnp.int32)
    hits = jnp.zeros((slot_total, slot_table[0].shape[0]), jnp.float32)
    for table in slot_table:
        hits = hits + jnp.sum(
            (table[None, :, :] == slot_ids[:, None, None]).astype(jnp.float32), axis=2
        )
    placed = jnp.dot(
        hits.astype(jnp.bfloat16), normalized_input, preferred_element_type=jnp.float32
    )
    return placed.astype(jnp.bfloat16)


def collect_rows(slot_table, slot_total, weights, gathered):
    slot_ids = jnp.arange(slot_total, dtype=jnp.int32)
    combine = jnp.zeros((weights.shape[0], slot_total), jnp.float32)
    for table in slot_table:
        combine = combine + jnp.sum(
            jnp.where(table[:, :, None] == slot_ids[None, None, :], weights[:, :, None], 0.0),
            axis=1,
        )
    upper_part = combine.astype(jnp.bfloat16)
    lower_part = (combine - upper_part.astype(jnp.float32)).astype(jnp.bfloat16)
    return jnp.dot(upper_part, gathered, preferred_element_type=jnp.float32) + jnp.dot(
        lower_part, gathered, preferred_element_type=jnp.float32
    )


def on_device(
    layer_hidden_input,
    norm_scale_vector,
    expert_choice_index,
    expert_choice_weight,
    request_of_token,
    adapter_of_request,
    adapter_of_slot,
    expert_gate_up_weight,
    expert_down_weight,
    adapter_down_weight,
    adapter_up_weight,
):
    tok_rows, model_width = layer_hidden_input.shape
    top_count = expert_choice_index.shape[1]
    pg_size = lax.axis_size(PG_AXES)
    expert_count = pg_size // 2
    slot_cap = 4 * tok_rows * top_count // (3 * expert_count)
    half_width = model_width // lax.axis_size("kv")
    kv_index = lax.axis_index("kv")
    normalized_input = normalize(layer_hidden_input, norm_scale_vector)
    own_features = lax.dynamic_slice_in_dim(normalized_input, kv_index * half_width, half_width, axis=1)
    down_own = lax.dynamic_slice_in_dim(adapter_down_weight[0], kv_index * half_width, half_width, axis=0)
    rank_half = down_own.shape[1]
    packed = jnp.concatenate([down_own.T, adapter_up_weight[0]], axis=0)
    flat_ids = expert_choice_index.reshape(-1)
    slot_rank = rank_in_expert(flat_ids, expert_count)
    rank_table = slot_rank.reshape(tok_rows, top_count)
    first_slot = 2 * expert_choice_index * slot_cap + rank_table
    second_slot = first_slot + slot_cap
    slot_total = pg_size * slot_cap
    outbox = place_rows((first_slot, second_slot), slot_total, own_features).reshape(
        pg_size, slot_cap, half_width
    )
    inbox_half = lax.all_to_all(outbox, PG_AXES, split_axis=0, concat_axis=0, tiled=True)
    packed_all = lax.all_gather(packed, PG_AXES, axis=0, tiled=False)
    weights = split_weights(expert_gate_up_weight, expert_down_weight, half_width)
    inbox_half, packed_all, weights = lax.optimization_barrier((inbox_half, packed_all, weights))
    half_out = expert_half(inbox_half.reshape(pg_size * slot_cap, half_width), weights)
    results = lax.all_to_all(
        half_out.reshape(pg_size, slot_cap, half_width),
        PG_AXES,
        split_axis=0,
        concat_axis=0,
        tiled=True,
    )
    moe_sum = collect_rows(
        (first_slot, second_slot),
        slot_total,
        expert_choice_weight,
        results.reshape(slot_total, half_width),
    )
    request_count = adapter_of_request.shape[0]
    owner_table = request_of_token[:, None] == jnp.arange(request_count, dtype=jnp.int32)[None, :]
    token_adapter = jnp.sum(jnp.where(owner_table, adapter_of_request[None, :], 0), axis=1)
    slot_count = packed_all.shape[0]
    down_all = packed_all[:, 0:rank_half, :].reshape(slot_count * rank_half, half_width)
    up_all = packed_all[:, rank_half:, :].reshape(slot_count * rank_half, half_width)
    partial_rank = lax.dot_general(
        own_features, down_all, (((1,), (1,)), ((), ())), preferred_element_type=jnp.float32
    )
    rank_projected = lax.psum(partial_rank, "kv").reshape(tok_rows, slot_count, rank_half)
    matched = adapter_of_slot[None, :, None] == token_adapter[:, None, None]
    rank_projected = jnp.where(matched, rank_projected, 0.0).astype(jnp.bfloat16)
    flat_low = rank_projected.reshape(tok_rows, slot_count * rank_half)
    adapter_total_output = jnp.dot(flat_low, up_all, preferred_element_type=jnp.float32)
    return (moe_sum + adapter_total_output).astype(jnp.bfloat16)


def solution(mesh):
    kv_count = mesh.shape["kv"]
    pg_count = mesh.shape["pg"]
    y_count = 4 if pg_count % 4 == 0 else 1
    rest = pg_count // y_count
    z_count = 8 if rest % 8 == 0 else rest
    x_count = rest // z_count
    split_mesh = jax.sharding.Mesh(
        mesh.devices.reshape(kv_count, x_count, z_count, y_count), ("kv",) + PG_AXES
    )
    pg = PG_AXES
    placed = (
        P(pg, None),
        P(),
        P(pg, None),
        P(pg, None),
        P(pg),
        P(),
        P(),
        P(pg, None, None, "kv"),
        P(pg, "kv", None),
        P(pg, None, None),
        P(pg, None, "kv"),
    )
    return jax.shard_map(
        on_device, mesh=split_mesh, in_specs=placed, out_specs=P(pg, "kv"), check_vma=False
    )
```

```python
import jax
import jax.numpy as jnp
from jax import lax
from jax.sharding import PartitionSpec as P


PG_AXES = ("px", "pz", "py")


def normalize(states, gain_vector):
    values = states.astype(jnp.float32)
    inverse_rms = lax.rsqrt(jnp.mean(values * values, axis=-1, keepdims=True) + 1e-06)
    return (values * inverse_rms * gain_vector).astype(jnp.bfloat16)


def swap_kv(values):
    return lax.ppermute(values, "kv", perm=[(0, 1), (1, 0)])


def expert_half(own_rows, weights):
    own_weight, other_weight, own_cols, other_cols = weights
    other_rows = swap_kv(own_rows)
    gate_up = jnp.einsum(
        "rd,dgf->rgf", own_rows, own_weight, preferred_element_type=jnp.float32
    ) + jnp.einsum("rd,dgf->rgf", other_rows, other_weight, preferred_element_type=jnp.float32)
    hidden = (jax.nn.silu(gate_up[:, 0]) * gate_up[:, 1]).astype(jnp.bfloat16)
    sent_quarter = jnp.dot(hidden, other_cols, preferred_element_type=jnp.float32).astype(
        jnp.bfloat16
    )
    received_quarter = swap_kv(sent_quarter)
    own_quarter = jnp.dot(hidden, own_cols, preferred_element_type=jnp.float32).astype(
        jnp.bfloat16
    )
    own_quarter, received_quarter = lax.optimization_barrier((own_quarter, received_quarter))
    return (own_quarter.astype(jnp.float32) + received_quarter.astype(jnp.float32)).astype(
        jnp.bfloat16
    )


def split_weights(expert_gate_up_weight, expert_down_weight, half_width):
    kv_index = lax.axis_index("kv")
    gate_up_weight = expert_gate_up_weight[0]
    own_weight = lax.dynamic_slice_in_dim(gate_up_weight, kv_index * half_width, half_width, 0)
    other_weight = lax.dynamic_slice_in_dim(
        gate_up_weight, (1 - kv_index) * half_width, half_width, 0
    )
    down_weight = expert_down_weight[0]
    own_cols = lax.dynamic_slice_in_dim(down_weight, kv_index * half_width, half_width, 1)
    other_cols = lax.dynamic_slice_in_dim(down_weight, (1 - kv_index) * half_width, half_width, 1)
    return own_weight, other_weight, own_cols, other_cols


def rank_in_expert(flat_ids, expert_count):
    onehot = (flat_ids[:, None] == jnp.arange(expert_count, dtype=jnp.int32)[None, :]).astype(
        jnp.bfloat16
    )
    entries = flat_ids.shape[0]
    lower = (
        jnp.arange(entries, dtype=jnp.int32)[:, None]
        >= jnp.arange(entries, dtype=jnp.int32)[None, :]
    ).astype(jnp.bfloat16)
    running = jnp.dot(lower, onehot, preferred_element_type=jnp.float32)
    return (jnp.sum(running * onehot.astype(jnp.float32), axis=1) - 1.0).astype(jnp.int32)


def place_rows(slot_table, slot_total, normalized_input):
    slot_ids = jnp.arange(slot_total, dtype=jnp.int32)
    hits = jnp.zeros((slot_total, slot_table[0].shape[0]), jnp.float32)
    for table in slot_table:
        hits = hits + jnp.sum(
            (table[None, :, :] == slot_ids[:, None, None]).astype(jnp.float32), axis=2
        )
    placed = jnp.dot(
        hits.astype(jnp.bfloat16), normalized_input, preferred_element_type=jnp.float32
    )
    return placed.astype(jnp.bfloat16)


def collect_rows(slot_table, slot_total, weights, gathered):
    slot_ids = jnp.arange(slot_total, dtype=jnp.int32)
    combine = jnp.zeros((weights.shape[0], slot_total), jnp.float32)
    for table in slot_table:
        combine = combine + jnp.sum(
            jnp.where(table[:, :, None] == slot_ids[None, None, :], weights[:, :, None], 0.0),
            axis=1,
        )
    upper_part = combine.astype(jnp.bfloat16)
    lower_part = (combine - upper_part.astype(jnp.float32)).astype(jnp.bfloat16)
    return jnp.dot(upper_part, gathered, preferred_element_type=jnp.float32) + jnp.dot(
        lower_part, gathered, preferred_element_type=jnp.float32
    )


def on_device(
    layer_hidden_input,
    norm_scale_vector,
    expert_choice_index,
    expert_choice_weight,
    request_of_token,
    adapter_of_request,
    adapter_of_slot,
    expert_gate_up_weight,
    expert_down_weight,
    adapter_down_weight,
    adapter_up_weight,
):
    tok_rows, model_width = layer_hidden_input.shape
    top_count = expert_choice_index.shape[1]
    pg_size = lax.axis_size(PG_AXES)
    expert_count = pg_size // 2
    slot_cap = 4 * tok_rows * top_count // (3 * expert_count)
    half_width = model_width // lax.axis_size("kv")
    kv_index = lax.axis_index("kv")
    normalized_input = normalize(layer_hidden_input, norm_scale_vector)
    own_features = lax.dynamic_slice_in_dim(normalized_input, kv_index * half_width, half_width, axis=1)
    down_own = lax.dynamic_slice_in_dim(adapter_down_weight[0], kv_index * half_width, half_width, axis=0)
    rank_half = down_own.shape[1]
    packed = jnp.concatenate([down_own.T, adapter_up_weight[0]], axis=0)
    flat_ids = expert_choice_index.reshape(-1)
    slot_rank = rank_in_expert(flat_ids, expert_count)
    rank_table = slot_rank.reshape(tok_rows, top_count)
    first_slot = 2 * expert_choice_index * slot_cap + rank_table
    second_slot = first_slot + slot_cap
    slot_total = pg_size * slot_cap
    outbox = place_rows((first_slot, second_slot), slot_total, own_features).reshape(
        pg_size, slot_cap, half_width
    )
    inbox_half = lax.all_to_all(outbox, PG_AXES, split_axis=0, concat_axis=0, tiled=True)
    packed_all = lax.all_gather(packed, PG_AXES[1:], axis=0, tiled=False)
    packed_all = lax.all_gather(packed_all, PG_AXES[0], axis=0, tiled=False)
    packed_all = packed_all.reshape((pg_size,) + packed.shape)
    weights = split_weights(expert_gate_up_weight, expert_down_weight, half_width)
    inbox_half, packed_all, weights = lax.optimization_barrier((inbox_half, packed_all, weights))
    half_out = expert_half(inbox_half.reshape(pg_size * slot_cap, half_width), weights)
    results = lax.all_to_all(
        half_out.reshape(pg_size, slot_cap, half_width),
        PG_AXES,
        split_axis=0,
        concat_axis=0,
        tiled=True,
    )
    moe_sum = collect_rows(
        (first_slot, second_slot),
        slot_total,
        expert_choice_weight,
        results.reshape(slot_total, half_width),
    )
    request_count = adapter_of_request.shape[0]
    owner_table = request_of_token[:, None] == jnp.arange(request_count, dtype=jnp.int32)[None, :]
    token_adapter = jnp.sum(jnp.where(owner_table, adapter_of_request[None, :], 0), axis=1)
    slot_count = packed_all.shape[0]
    down_all = packed_all[:, 0:rank_half, :].reshape(slot_count * rank_half, half_width)
    up_all = packed_all[:, rank_half:, :].reshape(slot_count * rank_half, half_width)
    partial_rank = lax.dot_general(
        own_features, down_all, (((1,), (1,)), ((), ())), preferred_element_type=jnp.float32
    )
    rank_projected = lax.psum(partial_rank, "kv").reshape(tok_rows, slot_count, rank_half)
    matched = adapter_of_slot[None, :, None] == token_adapter[:, None, None]
    rank_projected = jnp.where(matched, rank_projected, 0.0).astype(jnp.bfloat16)
    flat_low = rank_projected.reshape(tok_rows, slot_count * rank_half)
    adapter_total_output = jnp.dot(flat_low, up_all, preferred_element_type=jnp.float32)
    return (moe_sum + adapter_total_output).astype(jnp.bfloat16)


def solution(mesh):
    kv_count = mesh.shape["kv"]
    pg_count = mesh.shape["pg"]
    y_count = 4 if pg_count % 4 == 0 else 1
    rest = pg_count // y_count
    z_count = 8 if rest % 8 == 0 else rest
    x_count = rest // z_count
    split_mesh = jax.sharding.Mesh(
        mesh.devices.reshape(kv_count, x_count, z_count, y_count), ("kv",) + PG_AXES
    )
    pg = PG_AXES
    placed = (
        P(pg, None),
        P(),
        P(pg, None),
        P(pg, None),
        P(pg),
        P(),
        P(),
        P(pg, None, None, "kv"),
        P(pg, "kv", None),
        P(pg, None, None),
        P(pg, None, "kv"),
    )
    return jax.shard_map(
        on_device, mesh=split_mesh, in_specs=placed, out_specs=P(pg, "kv"), check_vma=False
    )
```

```python
import jax
import jax.numpy as jnp
from jax import lax
from jax.sharding import PartitionSpec as P


PG_AXES = ("px", "pz", "py")


def normalize(states, gain_vector):
    values = states.astype(jnp.float32)
    inverse_rms = lax.rsqrt(jnp.mean(values * values, axis=-1, keepdims=True) + 1e-06)
    return (values * inverse_rms * gain_vector).astype(jnp.bfloat16)


def swap_kv(values):
    return lax.ppermute(values, "kv", perm=[(0, 1), (1, 0)])


def expert_half(own_rows, weights):
    own_weight, other_weight, own_cols, other_cols = weights
    other_rows = swap_kv(own_rows)
    gate_up = jnp.einsum(
        "rd,dgf->rgf", own_rows, own_weight, preferred_element_type=jnp.float32
    ) + jnp.einsum("rd,dgf->rgf", other_rows, other_weight, preferred_element_type=jnp.float32)
    hidden = (jax.nn.silu(gate_up[:, 0]) * gate_up[:, 1]).astype(jnp.bfloat16)
    sent_quarter = jnp.dot(hidden, other_cols, preferred_element_type=jnp.float32).astype(
        jnp.bfloat16
    )
    received_quarter = swap_kv(sent_quarter)
    own_quarter = jnp.dot(hidden, own_cols, preferred_element_type=jnp.float32).astype(
        jnp.bfloat16
    )
    own_quarter, received_quarter = lax.optimization_barrier((own_quarter, received_quarter))
    return (own_quarter.astype(jnp.float32) + received_quarter.astype(jnp.float32)).astype(
        jnp.bfloat16
    )


def split_weights(expert_gate_up_weight, expert_down_weight, half_width):
    kv_index = lax.axis_index("kv")
    gate_up_weight = expert_gate_up_weight[0]
    own_weight = lax.dynamic_slice_in_dim(gate_up_weight, kv_index * half_width, half_width, 0)
    other_weight = lax.dynamic_slice_in_dim(
        gate_up_weight, (1 - kv_index) * half_width, half_width, 0
    )
    down_weight = expert_down_weight[0]
    own_cols = lax.dynamic_slice_in_dim(down_weight, kv_index * half_width, half_width, 1)
    other_cols = lax.dynamic_slice_in_dim(down_weight, (1 - kv_index) * half_width, half_width, 1)
    return own_weight, other_weight, own_cols, other_cols


def rank_in_expert(flat_ids, expert_count):
    onehot = (flat_ids[:, None] == jnp.arange(expert_count, dtype=jnp.int32)[None, :]).astype(
        jnp.bfloat16
    )
    entries = flat_ids.shape[0]
    lower = (
        jnp.arange(entries, dtype=jnp.int32)[:, None]
        >= jnp.arange(entries, dtype=jnp.int32)[None, :]
    ).astype(jnp.bfloat16)
    running = jnp.dot(lower, onehot, preferred_element_type=jnp.float32)
    return (jnp.sum(running * onehot.astype(jnp.float32), axis=1) - 1.0).astype(jnp.int32)


def place_rows(slot_table, slot_total, normalized_input):
    slot_ids = jnp.arange(slot_total, dtype=jnp.int32)
    hits = jnp.zeros((slot_total, slot_table[0].shape[0]), jnp.float32)
    for table in slot_table:
        hits = hits + jnp.sum(
            (table[None, :, :] == slot_ids[:, None, None]).astype(jnp.float32), axis=2
        )
    placed = jnp.dot(
        hits.astype(jnp.bfloat16), normalized_input, preferred_element_type=jnp.float32
    )
    return placed.astype(jnp.bfloat16)


def collect_rows(slot_table, slot_total, weights, gathered):
    slot_ids = jnp.arange(slot_total, dtype=jnp.int32)
    combine = jnp.zeros((weights.shape[0], slot_total), jnp.float32)
    for table in slot_table:
        combine = combine + jnp.sum(
            jnp.where(table[:, :, None] == slot_ids[None, None, :], weights[:, :, None], 0.0),
            axis=1,
        )
    upper_part = combine.astype(jnp.bfloat16)
    lower_part = (combine - upper_part.astype(jnp.float32)).astype(jnp.bfloat16)
    return jnp.dot(upper_part, gathered, preferred_element_type=jnp.float32) + jnp.dot(
        lower_part, gathered, preferred_element_type=jnp.float32
    )


def on_device(
    layer_hidden_input,
    norm_scale_vector,
    expert_choice_index,
    expert_choice_weight,
    request_of_token,
    adapter_of_request,
    adapter_of_slot,
    expert_gate_up_weight,
    expert_down_weight,
    adapter_down_weight,
    adapter_up_weight,
):
    tok_rows, model_width = layer_hidden_input.shape
    top_count = expert_choice_index.shape[1]
    pg_size = lax.axis_size(PG_AXES)
    expert_count = pg_size // 2
    slot_cap = 4 * tok_rows * top_count // (3 * expert_count)
    half_width = model_width // lax.axis_size("kv")
    kv_index = lax.axis_index("kv")
    normalized_input = normalize(layer_hidden_input, norm_scale_vector)
    own_features = lax.dynamic_slice_in_dim(normalized_input, kv_index * half_width, half_width, axis=1)
    down_own = lax.dynamic_slice_in_dim(adapter_down_weight[0], kv_index * half_width, half_width, axis=0)
    rank_half = down_own.shape[1]
    flat_ids = expert_choice_index.reshape(-1)
    slot_rank = rank_in_expert(flat_ids, expert_count)
    rank_table = slot_rank.reshape(tok_rows, top_count)
    first_slot = 2 * expert_choice_index * slot_cap + rank_table
    second_slot = first_slot + slot_cap
    slot_total = pg_size * slot_cap
    outbox = place_rows((first_slot, second_slot), slot_total, own_features).reshape(
        pg_size, slot_cap, half_width
    )
    inbox_half = lax.all_to_all(outbox, PG_AXES, split_axis=0, concat_axis=0, tiled=True)
    down_gathered = lax.all_gather(down_own.T, PG_AXES, axis=0, tiled=False)
    weights = split_weights(expert_gate_up_weight, expert_down_weight, half_width)
    inbox_half, down_gathered, weights = lax.optimization_barrier(
        (inbox_half, down_gathered, weights)
    )
    half_out = expert_half(inbox_half.reshape(pg_size * slot_cap, half_width), weights)
    results = lax.all_to_all(
        half_out.reshape(pg_size, slot_cap, half_width),
        PG_AXES,
        split_axis=0,
        concat_axis=0,
        tiled=True,
    )
    moe_sum = collect_rows(
        (first_slot, second_slot),
        slot_total,
        expert_choice_weight,
        results.reshape(slot_total, half_width),
    )
    request_count = adapter_of_request.shape[0]
    owner_table = request_of_token[:, None] == jnp.arange(request_count, dtype=jnp.int32)[None, :]
    token_adapter = jnp.sum(jnp.where(owner_table, adapter_of_request[None, :], 0), axis=1)
    up_gathered = lax.all_gather(adapter_up_weight[0], PG_AXES, axis=0, tiled=False)
    slot_count = down_gathered.shape[0]
    down_all = down_gathered.reshape(slot_count * rank_half, half_width)
    up_all = up_gathered.reshape(slot_count * rank_half, half_width)
    partial_rank = lax.dot_general(
        own_features, down_all, (((1,), (1,)), ((), ())), preferred_element_type=jnp.float32
    )
    rank_projected = lax.psum(partial_rank, "kv").reshape(tok_rows, slot_count, rank_half)
    matched = adapter_of_slot[None, :, None] == token_adapter[:, None, None]
    rank_projected = jnp.where(matched, rank_projected, 0.0).astype(jnp.bfloat16)
    flat_low = rank_projected.reshape(tok_rows, slot_count * rank_half)
    adapter_total_output = jnp.dot(flat_low, up_all, preferred_element_type=jnp.float32)
    return (moe_sum + adapter_total_output).astype(jnp.bfloat16)


def solution(mesh):
    kv_count = mesh.shape["kv"]
    pg_count = mesh.shape["pg"]
    y_count = 4 if pg_count % 4 == 0 else 1
    rest = pg_count // y_count
    z_count = 8 if rest % 8 == 0 else rest
    x_count = rest // z_count
    split_mesh = jax.sharding.Mesh(
        mesh.devices.reshape(kv_count, x_count, z_count, y_count), ("kv",) + PG_AXES
    )
    pg = PG_AXES
    placed = (
        P(pg, None),
        P(),
        P(pg, None),
        P(pg, None),
        P(pg),
        P(),
        P(),
        P(pg, None, None, "kv"),
        P(pg, "kv", None),
        P(pg, None, None),
        P(pg, None, "kv"),
    )
    return jax.shard_map(
        on_device, mesh=split_mesh, in_specs=placed, out_specs=P(pg, "kv"), check_vma=False
    )
```

```python
import jax
import jax.numpy as jnp
from jax import lax
from jax.sharding import PartitionSpec as P


PG_AXES = ("px", "pz", "py")


def normalize(states, gain_vector):
    values = states.astype(jnp.float32)
    inverse_rms = lax.rsqrt(jnp.mean(values * values, axis=-1, keepdims=True) + 1e-06)
    return (values * inverse_rms * gain_vector).astype(jnp.bfloat16)


def shift_gather(block, axis_name):
    count = lax.axis_size(axis_name)
    pieces = [block]
    for shift in range(1, count):
        pieces.append(
            lax.ppermute(
                block, axis_name, perm=[(j, (j + shift) % count) for j in range(count)]
            )
        )
    return jnp.stack(pieces)


def gathered_slot_order():
    x_axis, z_axis, y_axis = PG_AXES
    y_count = lax.axis_size(y_axis)
    x_ids = jnp.arange(lax.axis_size(x_axis), dtype=jnp.int32)
    z_ids = jnp.arange(lax.axis_size(z_axis), dtype=jnp.int32)
    y_src = (lax.axis_index(y_axis).astype(jnp.int32) - jnp.arange(y_count, dtype=jnp.int32)) % y_count
    z_count = z_ids.shape[0]
    slot = (x_ids[:, None, None] * z_count + z_ids[None, :, None]) * y_count + y_src[None, None, :]
    return slot.reshape(-1)


def swap_kv(values):
    return lax.ppermute(values, "kv", perm=[(0, 1), (1, 0)])


def expert_half(own_rows, weights):
    own_weight, other_weight, own_cols, other_cols = weights
    other_rows = swap_kv(own_rows)
    gate_up = jnp.einsum(
        "rd,dgf->rgf", own_rows, own_weight, preferred_element_type=jnp.float32
    ) + jnp.einsum("rd,dgf->rgf", other_rows, other_weight, preferred_element_type=jnp.float32)
    hidden = (jax.nn.silu(gate_up[:, 0]) * gate_up[:, 1]).astype(jnp.bfloat16)
    sent_quarter = jnp.dot(hidden, other_cols, preferred_element_type=jnp.float32).astype(
        jnp.bfloat16
    )
    received_quarter = swap_kv(sent_quarter)
    own_quarter = jnp.dot(hidden, own_cols, preferred_element_type=jnp.float32).astype(
        jnp.bfloat16
    )
    own_quarter, received_quarter = lax.optimization_barrier((own_quarter, received_quarter))
    return (own_quarter.astype(jnp.float32) + received_quarter.astype(jnp.float32)).astype(
        jnp.bfloat16
    )


def split_weights(expert_gate_up_weight, expert_down_weight, half_width):
    kv_index = lax.axis_index("kv")
    gate_up_weight = expert_gate_up_weight[0]
    own_weight = lax.dynamic_slice_in_dim(gate_up_weight, kv_index * half_width, half_width, 0)
    other_weight = lax.dynamic_slice_in_dim(
        gate_up_weight, (1 - kv_index) * half_width, half_width, 0
    )
    down_weight = expert_down_weight[0]
    own_cols = lax.dynamic_slice_in_dim(down_weight, kv_index * half_width, half_width, 1)
    other_cols = lax.dynamic_slice_in_dim(down_weight, (1 - kv_index) * half_width, half_width, 1)
    return own_weight, other_weight, own_cols, other_cols


def rank_in_expert(flat_ids, expert_count):
    onehot = (flat_ids[:, None] == jnp.arange(expert_count, dtype=jnp.int32)[None, :]).astype(
        jnp.bfloat16
    )
    entries = flat_ids.shape[0]
    lower = (
        jnp.arange(entries, dtype=jnp.int32)[:, None]
        >= jnp.arange(entries, dtype=jnp.int32)[None, :]
    ).astype(jnp.bfloat16)
    running = jnp.dot(lower, onehot, preferred_element_type=jnp.float32)
    return (jnp.sum(running * onehot.astype(jnp.float32), axis=1) - 1.0).astype(jnp.int32)


def place_rows(slot_table, slot_total, normalized_input):
    slot_ids = jnp.arange(slot_total, dtype=jnp.int32)
    hits = jnp.zeros((slot_total, slot_table[0].shape[0]), jnp.float32)
    for table in slot_table:
        hits = hits + jnp.sum(
            (table[None, :, :] == slot_ids[:, None, None]).astype(jnp.float32), axis=2
        )
    placed = jnp.dot(
        hits.astype(jnp.bfloat16), normalized_input, preferred_element_type=jnp.float32
    )
    return placed.astype(jnp.bfloat16)


def collect_rows(slot_table, slot_total, weights, gathered):
    slot_ids = jnp.arange(slot_total, dtype=jnp.int32)
    combine = jnp.zeros((weights.shape[0], slot_total), jnp.float32)
    for table in slot_table:
        combine = combine + jnp.sum(
            jnp.where(table[:, :, None] == slot_ids[None, None, :], weights[:, :, None], 0.0),
            axis=1,
        )
    upper_part = combine.astype(jnp.bfloat16)
    lower_part = (combine - upper_part.astype(jnp.float32)).astype(jnp.bfloat16)
    return jnp.dot(upper_part, gathered, preferred_element_type=jnp.float32) + jnp.dot(
        lower_part, gathered, preferred_element_type=jnp.float32
    )


def on_device(
    layer_hidden_input,
    norm_scale_vector,
    expert_choice_index,
    expert_choice_weight,
    request_of_token,
    adapter_of_request,
    adapter_of_slot,
    expert_gate_up_weight,
    expert_down_weight,
    adapter_down_weight,
    adapter_up_weight,
):
    tok_rows, model_width = layer_hidden_input.shape
    top_count = expert_choice_index.shape[1]
    pg_size = lax.axis_size(PG_AXES)
    expert_count = pg_size // 2
    slot_cap = 4 * tok_rows * top_count // (3 * expert_count)
    half_width = model_width // lax.axis_size("kv")
    kv_index = lax.axis_index("kv")
    normalized_input = normalize(layer_hidden_input, norm_scale_vector)
    own_features = lax.dynamic_slice_in_dim(normalized_input, kv_index * half_width, half_width, axis=1)
    down_own = lax.dynamic_slice_in_dim(adapter_down_weight[0], kv_index * half_width, half_width, axis=0)
    rank_half = down_own.shape[1]
    packed = jnp.concatenate([down_own.T, adapter_up_weight[0]], axis=0)
    flat_ids = expert_choice_index.reshape(-1)
    slot_rank = rank_in_expert(flat_ids, expert_count)
    rank_table = slot_rank.reshape(tok_rows, top_count)
    first_slot = 2 * expert_choice_index * slot_cap + rank_table
    second_slot = first_slot + slot_cap
    slot_total = pg_size * slot_cap
    outbox = place_rows((first_slot, second_slot), slot_total, own_features).reshape(
        pg_size, slot_cap, half_width
    )
    packed_near = shift_gather(packed, PG_AXES[2])
    outbox, packed_near = lax.optimization_barrier((outbox, packed_near))
    inbox_half = lax.all_to_all(outbox, PG_AXES, split_axis=0, concat_axis=0, tiled=True)
    packed_all = lax.all_gather(packed_near, PG_AXES[1], axis=0, tiled=False)
    packed_all = lax.all_gather(packed_all, PG_AXES[0], axis=0, tiled=False)
    packed_all = packed_all.reshape((pg_size,) + packed.shape)
    adapter_of_position = adapter_of_slot[gathered_slot_order()]
    weights = split_weights(expert_gate_up_weight, expert_down_weight, half_width)
    inbox_half, packed_all, weights = lax.optimization_barrier((inbox_half, packed_all, weights))
    half_out = expert_half(inbox_half.reshape(pg_size * slot_cap, half_width), weights)
    results = lax.all_to_all(
        half_out.reshape(pg_size, slot_cap, half_width),
        PG_AXES,
        split_axis=0,
        concat_axis=0,
        tiled=True,
    )
    moe_sum = collect_rows(
        (first_slot, second_slot),
        slot_total,
        expert_choice_weight,
        results.reshape(slot_total, half_width),
    )
    request_count = adapter_of_request.shape[0]
    owner_table = request_of_token[:, None] == jnp.arange(request_count, dtype=jnp.int32)[None, :]
    token_adapter = jnp.sum(jnp.where(owner_table, adapter_of_request[None, :], 0), axis=1)
    slot_count = packed_all.shape[0]
    down_all = packed_all[:, 0:rank_half, :].reshape(slot_count * rank_half, half_width)
    up_all = packed_all[:, rank_half:, :].reshape(slot_count * rank_half, half_width)
    partial_rank = lax.dot_general(
        own_features, down_all, (((1,), (1,)), ((), ())), preferred_element_type=jnp.float32
    )
    rank_projected = lax.psum(partial_rank, "kv").reshape(tok_rows, slot_count, rank_half)
    matched = adapter_of_position[None, :, None] == token_adapter[:, None, None]
    rank_projected = jnp.where(matched, rank_projected, 0.0).astype(jnp.bfloat16)
    flat_low = rank_projected.reshape(tok_rows, slot_count * rank_half)
    adapter_total_output = jnp.dot(flat_low, up_all, preferred_element_type=jnp.float32)
    return (moe_sum + adapter_total_output).astype(jnp.bfloat16)


def solution(mesh):
    kv_count = mesh.shape["kv"]
    pg_count = mesh.shape["pg"]
    y_count = 4 if pg_count % 4 == 0 else 1
    rest = pg_count // y_count
    z_count = 8 if rest % 8 == 0 else rest
    x_count = rest // z_count
    split_mesh = jax.sharding.Mesh(
        mesh.devices.reshape(kv_count, x_count, z_count, y_count), ("kv",) + PG_AXES
    )
    pg = PG_AXES
    placed = (
        P(pg, None),
        P(),
        P(pg, None),
        P(pg, None),
        P(pg),
        P(),
        P(),
        P(pg, None, None, "kv"),
        P(pg, "kv", None),
        P(pg, None, None),
        P(pg, None, "kv"),
    )
    return jax.shard_map(
        on_device, mesh=split_mesh, in_specs=placed, out_specs=P(pg, "kv"), check_vma=False
    )
```

```python
import jax
import jax.numpy as jnp
from jax import lax
from jax.sharding import PartitionSpec as P


PG_AXES = ("px", "pz", "py")


def normalize(states, gain_vector):
    values = states.astype(jnp.float32)
    inverse_rms = lax.rsqrt(jnp.mean(values * values, axis=-1, keepdims=True) + 1e-06)
    return (values * inverse_rms * gain_vector).astype(jnp.bfloat16)


def swap_kv(values):
    return lax.ppermute(values, "kv", perm=[(0, 1), (1, 0)])


def expert_half(own_rows, weights):
    own_weight, other_weight, own_units_down, other_units_down = weights
    other_rows = swap_kv(own_rows)
    gate_up = jnp.einsum(
        "rd,dgf->rgf", own_rows, own_weight, preferred_element_type=jnp.float32
    ) + jnp.einsum("rd,dgf->rgf", other_rows, other_weight, preferred_element_type=jnp.float32)
    own_hidden = (jax.nn.silu(gate_up[:, 0]) * gate_up[:, 1]).astype(jnp.bfloat16)
    other_hidden = swap_kv(own_hidden)
    own_quarter = jnp.dot(own_hidden, own_units_down, preferred_element_type=jnp.float32).astype(
        jnp.bfloat16
    )
    other_quarter = jnp.dot(
        other_hidden, other_units_down, preferred_element_type=jnp.float32
    ).astype(jnp.bfloat16)
    own_quarter, other_quarter = lax.optimization_barrier((own_quarter, other_quarter))
    return (own_quarter.astype(jnp.float32) + other_quarter.astype(jnp.float32)).astype(
        jnp.bfloat16
    )


def split_weights(expert_gate_up_weight, expert_down_weight, half_width):
    kv_index = lax.axis_index("kv")
    gate_up_weight = expert_gate_up_weight[0]
    own_weight = lax.dynamic_slice_in_dim(gate_up_weight, kv_index * half_width, half_width, 0)
    other_weight = lax.dynamic_slice_in_dim(
        gate_up_weight, (1 - kv_index) * half_width, half_width, 0
    )
    down_weight = expert_down_weight[0]
    own_units_down = lax.dynamic_slice_in_dim(down_weight, kv_index * half_width, half_width, 1)
    lent_down = lax.dynamic_slice_in_dim(down_weight, (1 - kv_index) * half_width, half_width, 1)
    other_units_down = swap_kv(lent_down)
    return own_weight, other_weight, own_units_down, other_units_down


def rank_in_expert(flat_ids, expert_count):
    onehot = (flat_ids[:, None] == jnp.arange(expert_count, dtype=jnp.int32)[None, :]).astype(
        jnp.bfloat16
    )
    entries = flat_ids.shape[0]
    lower = (
        jnp.arange(entries, dtype=jnp.int32)[:, None]
        >= jnp.arange(entries, dtype=jnp.int32)[None, :]
    ).astype(jnp.bfloat16)
    running = jnp.dot(lower, onehot, preferred_element_type=jnp.float32)
    return (jnp.sum(running * onehot.astype(jnp.float32), axis=1) - 1.0).astype(jnp.int32)


def place_rows(slot_table, slot_total, normalized_input):
    slot_ids = jnp.arange(slot_total, dtype=jnp.int32)
    hits = jnp.zeros((slot_total, slot_table[0].shape[0]), jnp.float32)
    for table in slot_table:
        hits = hits + jnp.sum(
            (table[None, :, :] == slot_ids[:, None, None]).astype(jnp.float32), axis=2
        )
    placed = jnp.dot(
        hits.astype(jnp.bfloat16), normalized_input, preferred_element_type=jnp.float32
    )
    return placed.astype(jnp.bfloat16)


def collect_rows(slot_table, slot_total, weights, gathered):
    slot_ids = jnp.arange(slot_total, dtype=jnp.int32)
    combine = jnp.zeros((weights.shape[0], slot_total), jnp.float32)
    for table in slot_table:
        combine = combine + jnp.sum(
            jnp.where(table[:, :, None] == slot_ids[None, None, :], weights[:, :, None], 0.0),
            axis=1,
        )
    upper_part = combine.astype(jnp.bfloat16)
    lower_part = (combine - upper_part.astype(jnp.float32)).astype(jnp.bfloat16)
    return jnp.dot(upper_part, gathered, preferred_element_type=jnp.float32) + jnp.dot(
        lower_part, gathered, preferred_element_type=jnp.float32
    )


def on_device(
    layer_hidden_input,
    norm_scale_vector,
    expert_choice_index,
    expert_choice_weight,
    request_of_token,
    adapter_of_request,
    adapter_of_slot,
    expert_gate_up_weight,
    expert_down_weight,
    adapter_down_weight,
    adapter_up_weight,
):
    tok_rows, model_width = layer_hidden_input.shape
    top_count = expert_choice_index.shape[1]
    pg_size = lax.axis_size(PG_AXES)
    expert_count = pg_size // 2
    slot_cap = 4 * tok_rows * top_count // (3 * expert_count)
    half_width = model_width // lax.axis_size("kv")
    kv_index = lax.axis_index("kv")
    normalized_input = normalize(layer_hidden_input, norm_scale_vector)
    own_features = lax.dynamic_slice_in_dim(normalized_input, kv_index * half_width, half_width, axis=1)
    down_own = lax.dynamic_slice_in_dim(adapter_down_weight[0], kv_index * half_width, half_width, axis=0)
    rank_half = down_own.shape[1]
    packed = jnp.concatenate([down_own.T, adapter_up_weight[0]], axis=0)
    flat_ids = expert_choice_index.reshape(-1)
    slot_rank = rank_in_expert(flat_ids, expert_count)
    rank_table = slot_rank.reshape(tok_rows, top_count)
    first_slot = 2 * expert_choice_index * slot_cap + rank_table
    second_slot = first_slot + slot_cap
    slot_total = pg_size * slot_cap
    outbox = place_rows((first_slot, second_slot), slot_total, own_features).reshape(
        pg_size, slot_cap, half_width
    )
    inbox_half = lax.all_to_all(outbox, PG_AXES, split_axis=0, concat_axis=0, tiled=True)
    packed_all = lax.all_gather(packed, PG_AXES, axis=0, tiled=False)
    weights = split_weights(expert_gate_up_weight, expert_down_weight, half_width)
    inbox_half, packed_all, weights = lax.optimization_barrier((inbox_half, packed_all, weights))
    half_out = expert_half(inbox_half.reshape(pg_size * slot_cap, half_width), weights)
    results = lax.all_to_all(
        half_out.reshape(pg_size, slot_cap, half_width),
        PG_AXES,
        split_axis=0,
        concat_axis=0,
        tiled=True,
    )
    moe_sum = collect_rows(
        (first_slot, second_slot),
        slot_total,
        expert_choice_weight,
        results.reshape(slot_total, half_width),
    )
    request_count = adapter_of_request.shape[0]
    owner_table = request_of_token[:, None] == jnp.arange(request_count, dtype=jnp.int32)[None, :]
    token_adapter = jnp.sum(jnp.where(owner_table, adapter_of_request[None, :], 0), axis=1)
    slot_count = packed_all.shape[0]
    down_all = packed_all[:, 0:rank_half, :].reshape(slot_count * rank_half, half_width)
    up_all = packed_all[:, rank_half:, :].reshape(slot_count * rank_half, half_width)
    partial_rank = lax.dot_general(
        own_features, down_all, (((1,), (1,)), ((), ())), preferred_element_type=jnp.float32
    )
    rank_projected = lax.psum(partial_rank, "kv").reshape(tok_rows, slot_count, rank_half)
    matched = adapter_of_slot[None, :, None] == token_adapter[:, None, None]
    rank_projected = jnp.where(matched, rank_projected, 0.0).astype(jnp.bfloat16)
    flat_low = rank_projected.reshape(tok_rows, slot_count * rank_half)
    adapter_total_output = jnp.dot(flat_low, up_all, preferred_element_type=jnp.float32)
    return (moe_sum + adapter_total_output).astype(jnp.bfloat16)


def solution(mesh):
    kv_count = mesh.shape["kv"]
    pg_count = mesh.shape["pg"]
    y_count = 4 if pg_count % 4 == 0 else 1
    rest = pg_count // y_count
    z_count = 8 if rest % 8 == 0 else rest
    x_count = rest // z_count
    split_mesh = jax.sharding.Mesh(
        mesh.devices.reshape(kv_count, x_count, z_count, y_count), ("kv",) + PG_AXES
    )
    pg = PG_AXES
    placed = (
        P(pg, None),
        P(),
        P(pg, None),
        P(pg, None),
        P(pg),
        P(),
        P(),
        P(pg, None, None, "kv"),
        P(pg, "kv", None),
        P(pg, None, None),
        P(pg, None, "kv"),
    )
    return jax.shard_map(
        on_device, mesh=split_mesh, in_specs=placed, out_specs=P(pg, "kv"), check_vma=False
    )
```

```python
import jax
import jax.numpy as jnp
from jax import lax
from jax.sharding import PartitionSpec as P


PG_AXES = ("px", "pz", "py")


def normalize(states, gain_vector):
    values = states.astype(jnp.float32)
    inverse_rms = lax.rsqrt(jnp.mean(values * values, axis=-1, keepdims=True) + 1e-06)
    return (values * inverse_rms * gain_vector).astype(jnp.bfloat16)


def swap_kv(values):
    return lax.ppermute(values, "kv", perm=[(0, 1), (1, 0)])


def expert_half(own_rows, weights):
    own_weight, other_weight, own_units_down, other_units_down = weights
    other_rows = swap_kv(own_rows)
    own_partial = jnp.einsum(
        "rd,dgf->rgf", own_rows, own_weight, preferred_element_type=jnp.float32
    )
    own_partial, other_rows = lax.optimization_barrier((own_partial, other_rows))
    gate_up = own_partial + jnp.einsum(
        "rd,dgf->rgf", other_rows, other_weight, preferred_element_type=jnp.float32
    )
    own_hidden = (jax.nn.silu(gate_up[:, 0]) * gate_up[:, 1]).astype(jnp.bfloat16)
    other_hidden = swap_kv(own_hidden)
    own_quarter = jnp.dot(own_hidden, own_units_down, preferred_element_type=jnp.float32).astype(
        jnp.bfloat16
    )
    other_quarter = jnp.dot(
        other_hidden, other_units_down, preferred_element_type=jnp.float32
    ).astype(jnp.bfloat16)
    own_quarter, other_quarter = lax.optimization_barrier((own_quarter, other_quarter))
    return (own_quarter.astype(jnp.float32) + other_quarter.astype(jnp.float32)).astype(
        jnp.bfloat16
    )


def split_weights(expert_gate_up_weight, expert_down_weight, half_width):
    kv_index = lax.axis_index("kv")
    gate_up_weight = expert_gate_up_weight[0]
    own_weight = lax.dynamic_slice_in_dim(gate_up_weight, kv_index * half_width, half_width, 0)
    other_weight = lax.dynamic_slice_in_dim(
        gate_up_weight, (1 - kv_index) * half_width, half_width, 0
    )
    down_weight = expert_down_weight[0]
    own_units_down = lax.dynamic_slice_in_dim(down_weight, kv_index * half_width, half_width, 1)
    lent_down = lax.dynamic_slice_in_dim(down_weight, (1 - kv_index) * half_width, half_width, 1)
    other_units_down = swap_kv(lent_down)
    return own_weight, other_weight, own_units_down, other_units_down


def rank_in_expert(flat_ids, expert_count):
    onehot = (flat_ids[:, None] == jnp.arange(expert_count, dtype=jnp.int32)[None, :]).astype(
        jnp.bfloat16
    )
    entries = flat_ids.shape[0]
    lower = (
        jnp.arange(entries, dtype=jnp.int32)[:, None]
        >= jnp.arange(entries, dtype=jnp.int32)[None, :]
    ).astype(jnp.bfloat16)
    running = jnp.dot(lower, onehot, preferred_element_type=jnp.float32)
    return (jnp.sum(running * onehot.astype(jnp.float32), axis=1) - 1.0).astype(jnp.int32)


def place_rows(slot_table, slot_total, normalized_input):
    slot_ids = jnp.arange(slot_total, dtype=jnp.int32)
    hits = jnp.zeros((slot_total, slot_table[0].shape[0]), jnp.float32)
    for table in slot_table:
        hits = hits + jnp.sum(
            (table[None, :, :] == slot_ids[:, None, None]).astype(jnp.float32), axis=2
        )
    placed = jnp.dot(
        hits.astype(jnp.bfloat16), normalized_input, preferred_element_type=jnp.float32
    )
    return placed.astype(jnp.bfloat16)


def collect_rows(slot_table, slot_total, weights, gathered):
    slot_ids = jnp.arange(slot_total, dtype=jnp.int32)
    combine = jnp.zeros((weights.shape[0], slot_total), jnp.float32)
    for table in slot_table:
        combine = combine + jnp.sum(
            jnp.where(table[:, :, None] == slot_ids[None, None, :], weights[:, :, None], 0.0),
            axis=1,
        )
    upper_part = combine.astype(jnp.bfloat16)
    lower_part = (combine - upper_part.astype(jnp.float32)).astype(jnp.bfloat16)
    return jnp.dot(upper_part, gathered, preferred_element_type=jnp.float32) + jnp.dot(
        lower_part, gathered, preferred_element_type=jnp.float32
    )


def on_device(
    layer_hidden_input,
    norm_scale_vector,
    expert_choice_index,
    expert_choice_weight,
    request_of_token,
    adapter_of_request,
    adapter_of_slot,
    expert_gate_up_weight,
    expert_down_weight,
    adapter_down_weight,
    adapter_up_weight,
):
    tok_rows, model_width = layer_hidden_input.shape
    top_count = expert_choice_index.shape[1]
    pg_size = lax.axis_size(PG_AXES)
    expert_count = pg_size // 2
    slot_cap = 4 * tok_rows * top_count // (3 * expert_count)
    half_width = model_width // lax.axis_size("kv")
    kv_index = lax.axis_index("kv")
    normalized_input = normalize(layer_hidden_input, norm_scale_vector)
    own_features = lax.dynamic_slice_in_dim(normalized_input, kv_index * half_width, half_width, axis=1)
    down_own = lax.dynamic_slice_in_dim(adapter_down_weight[0], kv_index * half_width, half_width, axis=0)
    rank_half = down_own.shape[1]
    packed = jnp.concatenate([down_own.T, adapter_up_weight[0]], axis=0)
    flat_ids = expert_choice_index.reshape(-1)
    slot_rank = rank_in_expert(flat_ids, expert_count)
    rank_table = slot_rank.reshape(tok_rows, top_count)
    first_slot = 2 * expert_choice_index * slot_cap + rank_table
    second_slot = first_slot + slot_cap
    slot_total = pg_size * slot_cap
    outbox = place_rows((first_slot, second_slot), slot_total, own_features).reshape(
        pg_size, slot_cap, half_width
    )
    inbox_half = lax.all_to_all(outbox, PG_AXES, split_axis=0, concat_axis=0, tiled=True)
    packed_all = lax.all_gather(packed, PG_AXES, axis=0, tiled=False)
    weights = split_weights(expert_gate_up_weight, expert_down_weight, half_width)
    inbox_half, packed_all, weights = lax.optimization_barrier((inbox_half, packed_all, weights))
    half_out = expert_half(inbox_half.reshape(pg_size * slot_cap, half_width), weights)
    results = lax.all_to_all(
        half_out.reshape(pg_size, slot_cap, half_width),
        PG_AXES,
        split_axis=0,
        concat_axis=0,
        tiled=True,
    )
    moe_sum = collect_rows(
        (first_slot, second_slot),
        slot_total,
        expert_choice_weight,
        results.reshape(slot_total, half_width),
    )
    request_count = adapter_of_request.shape[0]
    owner_table = request_of_token[:, None] == jnp.arange(request_count, dtype=jnp.int32)[None, :]
    token_adapter = jnp.sum(jnp.where(owner_table, adapter_of_request[None, :], 0), axis=1)
    slot_count = packed_all.shape[0]
    down_all = packed_all[:, 0:rank_half, :].reshape(slot_count * rank_half, half_width)
    up_all = packed_all[:, rank_half:, :].reshape(slot_count * rank_half, half_width)
    partial_rank = lax.dot_general(
        own_features, down_all, (((1,), (1,)), ((), ())), preferred_element_type=jnp.float32
    )
    rank_projected = lax.psum(partial_rank, "kv").reshape(tok_rows, slot_count, rank_half)
    matched = adapter_of_slot[None, :, None] == token_adapter[:, None, None]
    rank_projected = jnp.where(matched, rank_projected, 0.0).astype(jnp.bfloat16)
    flat_low = rank_projected.reshape(tok_rows, slot_count * rank_half)
    adapter_total_output = jnp.dot(flat_low, up_all, preferred_element_type=jnp.float32)
    return (moe_sum + adapter_total_output).astype(jnp.bfloat16)


def solution(mesh):
    kv_count = mesh.shape["kv"]
    pg_count = mesh.shape["pg"]
    y_count = 4 if pg_count % 4 == 0 else 1
    rest = pg_count // y_count
    z_count = 8 if rest % 8 == 0 else rest
    x_count = rest // z_count
    split_mesh = jax.sharding.Mesh(
        mesh.devices.reshape(kv_count, x_count, z_count, y_count), ("kv",) + PG_AXES
    )
    pg = PG_AXES
    placed = (
        P(pg, None),
        P(),
        P(pg, None),
        P(pg, None),
        P(pg),
        P(),
        P(),
        P(pg, None, None, "kv"),
        P(pg, "kv", None),
        P(pg, None, None),
        P(pg, None, "kv"),
    )
    return jax.shard_map(
        on_device, mesh=split_mesh, in_specs=placed, out_specs=P(pg, "kv"), check_vma=False
    )
```

```python
import jax
import jax.numpy as jnp
from jax import lax
from jax.sharding import PartitionSpec as P


PG_AXES = ("px", "pz", "py")


def normalize(states, gain_vector):
    values = states.astype(jnp.float32)
    inverse_rms = lax.rsqrt(jnp.mean(values * values, axis=-1, keepdims=True) + 1e-06)
    return (values * inverse_rms * gain_vector).astype(jnp.bfloat16)


def swap_kv(values):
    return lax.ppermute(values, "kv", perm=[(0, 1), (1, 0)])


def expert_half(own_rows, weights):
    own_weight, other_weight, own_units_down, other_units_down = weights
    other_rows = swap_kv(own_rows)
    own_partial = jnp.einsum(
        "rd,dgf->rgf", own_rows, own_weight, preferred_element_type=jnp.float32
    )
    own_partial, other_rows = lax.optimization_barrier((own_partial, other_rows))
    gate_up = own_partial + jnp.einsum(
        "rd,dgf->rgf", other_rows, other_weight, preferred_element_type=jnp.float32
    )
    own_hidden = (jax.nn.silu(gate_up[:, 0]) * gate_up[:, 1]).astype(jnp.bfloat16)
    other_hidden = swap_kv(own_hidden)
    own_quarter = jnp.dot(own_hidden, own_units_down, preferred_element_type=jnp.float32).astype(
        jnp.bfloat16
    )
    other_quarter = jnp.dot(
        other_hidden, other_units_down, preferred_element_type=jnp.float32
    ).astype(jnp.bfloat16)
    own_quarter, other_quarter = lax.optimization_barrier((own_quarter, other_quarter))
    return (own_quarter.astype(jnp.float32) + other_quarter.astype(jnp.float32)).astype(
        jnp.bfloat16
    )


def split_weights(expert_gate_up_weight, expert_down_weight, half_width):
    kv_index = lax.axis_index("kv")
    gate_up_weight = expert_gate_up_weight[0]
    own_weight = lax.dynamic_slice_in_dim(gate_up_weight, kv_index * half_width, half_width, 0)
    other_weight = lax.dynamic_slice_in_dim(
        gate_up_weight, (1 - kv_index) * half_width, half_width, 0
    )
    down_weight = expert_down_weight[0]
    own_units_down = lax.dynamic_slice_in_dim(down_weight, kv_index * half_width, half_width, 1)
    lent_down = lax.dynamic_slice_in_dim(down_weight, (1 - kv_index) * half_width, half_width, 1)
    other_units_down = swap_kv(lent_down)
    return own_weight, other_weight, own_units_down, other_units_down


def rank_in_expert(flat_ids, expert_count):
    onehot = (flat_ids[:, None] == jnp.arange(expert_count, dtype=jnp.int32)[None, :]).astype(
        jnp.bfloat16
    )
    entries = flat_ids.shape[0]
    lower = (
        jnp.arange(entries, dtype=jnp.int32)[:, None]
        >= jnp.arange(entries, dtype=jnp.int32)[None, :]
    ).astype(jnp.bfloat16)
    running = jnp.dot(lower, onehot, preferred_element_type=jnp.float32)
    return (jnp.sum(running * onehot.astype(jnp.float32), axis=1) - 1.0).astype(jnp.int32)


def place_rows(slot_table, slot_total, normalized_input):
    token_count, width = normalized_input.shape
    token_ids = jnp.broadcast_to(
        jnp.arange(token_count, dtype=jnp.int32)[:, None], slot_table[0].shape
    ).reshape(-1)
    slot_token = jnp.full((slot_total,), token_count, jnp.int32)
    for table in slot_table:
        slot_token = slot_token.at[table.reshape(-1)].set(token_ids)
    padded = jnp.concatenate(
        [normalized_input, jnp.zeros((1, width), normalized_input.dtype)], axis=0
    )
    return jnp.take(padded, slot_token, axis=0)


def collect_rows(slot_table, slot_total, weights, gathered):
    slot_ids = jnp.arange(slot_total, dtype=jnp.int32)
    combine = jnp.zeros((weights.shape[0], slot_total), jnp.float32)
    for table in slot_table:
        combine = combine + jnp.sum(
            jnp.where(table[:, :, None] == slot_ids[None, None, :], weights[:, :, None], 0.0),
            axis=1,
        )
    upper_part = combine.astype(jnp.bfloat16)
    lower_part = (combine - upper_part.astype(jnp.float32)).astype(jnp.bfloat16)
    return jnp.dot(upper_part, gathered, preferred_element_type=jnp.float32) + jnp.dot(
        lower_part, gathered, preferred_element_type=jnp.float32
    )


def on_device(
    layer_hidden_input,
    norm_scale_vector,
    expert_choice_index,
    expert_choice_weight,
    request_of_token,
    adapter_of_request,
    adapter_of_slot,
    expert_gate_up_weight,
    expert_down_weight,
    adapter_down_weight,
    adapter_up_weight,
):
    tok_rows, model_width = layer_hidden_input.shape
    top_count = expert_choice_index.shape[1]
    pg_size = lax.axis_size(PG_AXES)
    expert_count = pg_size // 2
    slot_cap = 4 * tok_rows * top_count // (3 * expert_count)
    half_width = model_width // lax.axis_size("kv")
    kv_index = lax.axis_index("kv")
    normalized_input = normalize(layer_hidden_input, norm_scale_vector)
    own_features = lax.dynamic_slice_in_dim(normalized_input, kv_index * half_width, half_width, axis=1)
    down_own = lax.dynamic_slice_in_dim(adapter_down_weight[0], kv_index * half_width, half_width, axis=0)
    rank_half = down_own.shape[1]
    packed = jnp.concatenate([down_own.T, adapter_up_weight[0]], axis=0)
    flat_ids = expert_choice_index.reshape(-1)
    slot_rank = rank_in_expert(flat_ids, expert_count)
    rank_table = slot_rank.reshape(tok_rows, top_count)
    first_slot = 2 * expert_choice_index * slot_cap + rank_table
    second_slot = first_slot + slot_cap
    slot_total = pg_size * slot_cap
    outbox = place_rows((first_slot, second_slot), slot_total, own_features).reshape(
        pg_size, slot_cap, half_width
    )
    inbox_half = lax.all_to_all(outbox, PG_AXES, split_axis=0, concat_axis=0, tiled=True)
    packed_all = lax.all_gather(packed, PG_AXES, axis=0, tiled=False)
    weights = split_weights(expert_gate_up_weight, expert_down_weight, half_width)
    inbox_half, packed_all, weights = lax.optimization_barrier((inbox_half, packed_all, weights))
    half_out = expert_half(inbox_half.reshape(pg_size * slot_cap, half_width), weights)
    results = lax.all_to_all(
        half_out.reshape(pg_size, slot_cap, half_width),
        PG_AXES,
        split_axis=0,
        concat_axis=0,
        tiled=True,
    )
    moe_sum = collect_rows(
        (first_slot, second_slot),
        slot_total,
        expert_choice_weight,
        results.reshape(slot_total, half_width),
    )
    request_count = adapter_of_request.shape[0]
    owner_table = request_of_token[:, None] == jnp.arange(request_count, dtype=jnp.int32)[None, :]
    token_adapter = jnp.sum(jnp.where(owner_table, adapter_of_request[None, :], 0), axis=1)
    slot_count = packed_all.shape[0]
    down_all = packed_all[:, 0:rank_half, :].reshape(slot_count * rank_half, half_width)
    up_all = packed_all[:, rank_half:, :].reshape(slot_count * rank_half, half_width)
    partial_rank = lax.dot_general(
        own_features, down_all, (((1,), (1,)), ((), ())), preferred_element_type=jnp.float32
    )
    rank_projected = lax.psum(partial_rank, "kv").reshape(tok_rows, slot_count, rank_half)
    matched = adapter_of_slot[None, :, None] == token_adapter[:, None, None]
    rank_projected = jnp.where(matched, rank_projected, 0.0).astype(jnp.bfloat16)
    flat_low = rank_projected.reshape(tok_rows, slot_count * rank_half)
    adapter_total_output = jnp.dot(flat_low, up_all, preferred_element_type=jnp.float32)
    return (moe_sum + adapter_total_output).astype(jnp.bfloat16)


def solution(mesh):
    kv_count = mesh.shape["kv"]
    pg_count = mesh.shape["pg"]
    y_count = 4 if pg_count % 4 == 0 else 1
    rest = pg_count // y_count
    z_count = 8 if rest % 8 == 0 else rest
    x_count = rest // z_count
    split_mesh = jax.sharding.Mesh(
        mesh.devices.reshape(kv_count, x_count, z_count, y_count), ("kv",) + PG_AXES
    )
    pg = PG_AXES
    placed = (
        P(pg, None),
        P(),
        P(pg, None),
        P(pg, None),
        P(pg),
        P(),
        P(),
        P(pg, None, None, "kv"),
        P(pg, "kv", None),
        P(pg, None, None),
        P(pg, None, "kv"),
    )
    return jax.shard_map(
        on_device, mesh=split_mesh, in_specs=placed, out_specs=P(pg, "kv"), check_vma=False
    )
```

```python
import jax
import jax.numpy as jnp
from jax import lax
from jax.sharding import PartitionSpec as P


PG_AXES = ("px", "pz", "py")


def normalize(states, gain_vector):
    values = states.astype(jnp.float32)
    inverse_rms = lax.rsqrt(jnp.mean(values * values, axis=-1, keepdims=True) + 1e-06)
    return (values * inverse_rms * gain_vector).astype(jnp.bfloat16)


def swap_kv(values):
    return lax.ppermute(values, "kv", perm=[(0, 1), (1, 0)])


def expert_half(own_rows, weights):
    own_weight, other_weight, own_units_down, other_units_down = weights
    other_rows = swap_kv(own_rows)
    own_partial = jnp.einsum(
        "rd,dgf->rgf", own_rows, own_weight, preferred_element_type=jnp.float32
    )
    own_partial, other_rows = lax.optimization_barrier((own_partial, other_rows))
    gate_up = own_partial + jnp.einsum(
        "rd,dgf->rgf", other_rows, other_weight, preferred_element_type=jnp.float32
    )
    own_hidden = (jax.nn.silu(gate_up[:, 0]) * gate_up[:, 1]).astype(jnp.bfloat16)
    other_hidden = swap_kv(own_hidden)
    own_quarter = jnp.dot(own_hidden, own_units_down, preferred_element_type=jnp.float32).astype(
        jnp.bfloat16
    )
    own_quarter, other_hidden = lax.optimization_barrier((own_quarter, other_hidden))
    other_quarter = jnp.dot(
        other_hidden, other_units_down, preferred_element_type=jnp.float32
    ).astype(jnp.bfloat16)
    return (own_quarter.astype(jnp.float32) + other_quarter.astype(jnp.float32)).astype(
        jnp.bfloat16
    )


def split_weights(expert_gate_up_weight, expert_down_weight, half_width):
    kv_index = lax.axis_index("kv")
    gate_up_weight = expert_gate_up_weight[0]
    own_weight = lax.dynamic_slice_in_dim(gate_up_weight, kv_index * half_width, half_width, 0)
    other_weight = lax.dynamic_slice_in_dim(
        gate_up_weight, (1 - kv_index) * half_width, half_width, 0
    )
    down_weight = expert_down_weight[0]
    own_units_down = lax.dynamic_slice_in_dim(down_weight, kv_index * half_width, half_width, 1)
    lent_down = lax.dynamic_slice_in_dim(down_weight, (1 - kv_index) * half_width, half_width, 1)
    other_units_down = swap_kv(lent_down)
    return own_weight, other_weight, own_units_down, other_units_down


def rank_in_expert(flat_ids, expert_count):
    onehot = (flat_ids[:, None] == jnp.arange(expert_count, dtype=jnp.int32)[None, :]).astype(
        jnp.bfloat16
    )
    entries = flat_ids.shape[0]
    lower = (
        jnp.arange(entries, dtype=jnp.int32)[:, None]
        >= jnp.arange(entries, dtype=jnp.int32)[None, :]
    ).astype(jnp.bfloat16)
    running = jnp.dot(lower, onehot, preferred_element_type=jnp.float32)
    return (jnp.sum(running * onehot.astype(jnp.float32), axis=1) - 1.0).astype(jnp.int32)


def place_rows(slot_table, slot_total, normalized_input):
    slot_ids = jnp.arange(slot_total, dtype=jnp.int32)
    hits = jnp.zeros((slot_total, slot_table[0].shape[0]), jnp.float32)
    for table in slot_table:
        hits = hits + jnp.sum(
            (table[None, :, :] == slot_ids[:, None, None]).astype(jnp.float32), axis=2
        )
    placed = jnp.dot(
        hits.astype(jnp.bfloat16), normalized_input, preferred_element_type=jnp.float32
    )
    return placed.astype(jnp.bfloat16)


def collect_rows(slot_table, slot_total, weights, gathered):
    slot_ids = jnp.arange(slot_total, dtype=jnp.int32)
    combine = jnp.zeros((weights.shape[0], slot_total), jnp.float32)
    for table in slot_table:
        combine = combine + jnp.sum(
            jnp.where(table[:, :, None] == slot_ids[None, None, :], weights[:, :, None], 0.0),
            axis=1,
        )
    upper_part = combine.astype(jnp.bfloat16)
    lower_part = (combine - upper_part.astype(jnp.float32)).astype(jnp.bfloat16)
    return jnp.dot(upper_part, gathered, preferred_element_type=jnp.float32) + jnp.dot(
        lower_part, gathered, preferred_element_type=jnp.float32
    )


def on_device(
    layer_hidden_input,
    norm_scale_vector,
    expert_choice_index,
    expert_choice_weight,
    request_of_token,
    adapter_of_request,
    adapter_of_slot,
    expert_gate_up_weight,
    expert_down_weight,
    adapter_down_weight,
    adapter_up_weight,
):
    tok_rows, model_width = layer_hidden_input.shape
    top_count = expert_choice_index.shape[1]
    pg_size = lax.axis_size(PG_AXES)
    expert_count = pg_size // 2
    slot_cap = 4 * tok_rows * top_count // (3 * expert_count)
    half_width = model_width // lax.axis_size("kv")
    kv_index = lax.axis_index("kv")
    normalized_input = normalize(layer_hidden_input, norm_scale_vector)
    own_features = lax.dynamic_slice_in_dim(normalized_input, kv_index * half_width, half_width, axis=1)
    down_own = lax.dynamic_slice_in_dim(adapter_down_weight[0], kv_index * half_width, half_width, axis=0)
    rank_half = down_own.shape[1]
    packed = jnp.concatenate([down_own.T, adapter_up_weight[0]], axis=0)
    flat_ids = expert_choice_index.reshape(-1)
    slot_rank = rank_in_expert(flat_ids, expert_count)
    rank_table = slot_rank.reshape(tok_rows, top_count)
    first_slot = 2 * expert_choice_index * slot_cap + rank_table
    second_slot = first_slot + slot_cap
    slot_total = pg_size * slot_cap
    outbox = place_rows((first_slot, second_slot), slot_total, own_features).reshape(
        pg_size, slot_cap, half_width
    )
    inbox_half = lax.all_to_all(outbox, PG_AXES, split_axis=0, concat_axis=0, tiled=True)
    packed_all = lax.all_gather(packed, PG_AXES, axis=0, tiled=False)
    weights = split_weights(expert_gate_up_weight, expert_down_weight, half_width)
    inbox_half, packed_all, weights = lax.optimization_barrier((inbox_half, packed_all, weights))
    half_out = expert_half(inbox_half.reshape(pg_size * slot_cap, half_width), weights)
    results = lax.all_to_all(
        half_out.reshape(pg_size, slot_cap, half_width),
        PG_AXES,
        split_axis=0,
        concat_axis=0,
        tiled=True,
    )
    moe_sum = collect_rows(
        (first_slot, second_slot),
        slot_total,
        expert_choice_weight,
        results.reshape(slot_total, half_width),
    )
    request_count = adapter_of_request.shape[0]
    owner_table = request_of_token[:, None] == jnp.arange(request_count, dtype=jnp.int32)[None, :]
    token_adapter = jnp.sum(jnp.where(owner_table, adapter_of_request[None, :], 0), axis=1)
    slot_count = packed_all.shape[0]
    down_all = packed_all[:, 0:rank_half, :].reshape(slot_count * rank_half, half_width)
    up_all = packed_all[:, rank_half:, :].reshape(slot_count * rank_half, half_width)
    partial_rank = lax.dot_general(
        own_features, down_all, (((1,), (1,)), ((), ())), preferred_element_type=jnp.float32
    )
    rank_projected = lax.psum(partial_rank, "kv").reshape(tok_rows, slot_count, rank_half)
    matched = adapter_of_slot[None, :, None] == token_adapter[:, None, None]
    rank_projected = jnp.where(matched, rank_projected, 0.0).astype(jnp.bfloat16)
    flat_low = rank_projected.reshape(tok_rows, slot_count * rank_half)
    adapter_total_output = jnp.dot(flat_low, up_all, preferred_element_type=jnp.float32)
    return (moe_sum + adapter_total_output).astype(jnp.bfloat16)


def solution(mesh):
    kv_count = mesh.shape["kv"]
    pg_count = mesh.shape["pg"]
    y_count = 4 if pg_count % 4 == 0 else 1
    rest = pg_count // y_count
    z_count = 8 if rest % 8 == 0 else rest
    x_count = rest // z_count
    split_mesh = jax.sharding.Mesh(
        mesh.devices.reshape(kv_count, x_count, z_count, y_count), ("kv",) + PG_AXES
    )
    pg = PG_AXES
    placed = (
        P(pg, None),
        P(),
        P(pg, None),
        P(pg, None),
        P(pg),
        P(),
        P(),
        P(pg, None, None, "kv"),
        P(pg, "kv", None),
        P(pg, None, None),
        P(pg, None, "kv"),
    )
    return jax.shard_map(
        on_device, mesh=split_mesh, in_specs=placed, out_specs=P(pg, "kv"), check_vma=False
    )
```

```python
import jax
import jax.numpy as jnp
from jax import lax
from jax.sharding import PartitionSpec as P


PG_AXES = ("px", "pz", "py")


def normalize(states, gain_vector):
    values = states.astype(jnp.float32)
    inverse_rms = lax.rsqrt(jnp.mean(values * values, axis=-1, keepdims=True) + 1e-06)
    return (values * inverse_rms * gain_vector).astype(jnp.bfloat16)


def swap_kv(values):
    return lax.ppermute(values, "kv", perm=[(0, 1), (1, 0)])


def expert_half(own_rows, weights):
    own_weight, other_weight, own_units_down, other_units_down = weights
    other_rows = swap_kv(own_rows)
    own_partial = jnp.einsum(
        "rd,dgf->rgf", own_rows, own_weight, preferred_element_type=jnp.float32
    )
    own_partial, other_rows = lax.optimization_barrier((own_partial, other_rows))
    gate_up = own_partial + jnp.einsum(
        "rd,dgf->rgf", other_rows, other_weight, preferred_element_type=jnp.float32
    )
    own_hidden = (jax.nn.silu(gate_up[:, 0]) * gate_up[:, 1]).astype(jnp.bfloat16)
    other_hidden = swap_kv(own_hidden)
    own_quarter = jnp.dot(own_hidden, own_units_down, preferred_element_type=jnp.float32).astype(
        jnp.bfloat16
    )
    other_quarter = jnp.dot(
        other_hidden, other_units_down, preferred_element_type=jnp.float32
    ).astype(jnp.bfloat16)
    own_quarter, other_quarter = lax.optimization_barrier((own_quarter, other_quarter))
    return (own_quarter.astype(jnp.float32) + other_quarter.astype(jnp.float32)).astype(
        jnp.bfloat16
    )


def split_weights(expert_gate_up_weight, expert_down_weight, half_width):
    kv_index = lax.axis_index("kv")
    gate_up_weight = expert_gate_up_weight[0]
    own_weight = lax.dynamic_slice_in_dim(gate_up_weight, kv_index * half_width, half_width, 0)
    other_weight = lax.dynamic_slice_in_dim(
        gate_up_weight, (1 - kv_index) * half_width, half_width, 0
    )
    down_weight = expert_down_weight[0]
    own_units_down = lax.dynamic_slice_in_dim(down_weight, kv_index * half_width, half_width, 1)
    lent_down = lax.dynamic_slice_in_dim(down_weight, (1 - kv_index) * half_width, half_width, 1)
    other_units_down = swap_kv(lent_down)
    return own_weight, other_weight, own_units_down, other_units_down


def rank_in_expert(flat_ids, expert_count):
    onehot = (flat_ids[:, None] == jnp.arange(expert_count, dtype=jnp.int32)[None, :]).astype(
        jnp.bfloat16
    )
    entries = flat_ids.shape[0]
    lower = (
        jnp.arange(entries, dtype=jnp.int32)[:, None]
        >= jnp.arange(entries, dtype=jnp.int32)[None, :]
    ).astype(jnp.bfloat16)
    running = jnp.dot(lower, onehot, preferred_element_type=jnp.float32)
    return (jnp.sum(running * onehot.astype(jnp.float32), axis=1) - 1.0).astype(jnp.int32)


def place_rows(slot_table, slot_total, normalized_input):
    slot_ids = jnp.arange(slot_total, dtype=jnp.int32)
    hits = jnp.zeros((slot_total, slot_table[0].shape[0]), jnp.float32)
    for table in slot_table:
        hits = hits + jnp.sum(
            (table[None, :, :] == slot_ids[:, None, None]).astype(jnp.float32), axis=2
        )
    placed = jnp.dot(
        hits.astype(jnp.bfloat16), normalized_input, preferred_element_type=jnp.float32
    )
    return placed.astype(jnp.bfloat16)


def collect_rows(slot_table, slot_total, weights, gathered):
    slot_ids = jnp.arange(slot_total, dtype=jnp.int32)
    combine = jnp.zeros((weights.shape[0], slot_total), jnp.float32)
    for table in slot_table:
        combine = combine + jnp.sum(
            jnp.where(table[:, :, None] == slot_ids[None, None, :], weights[:, :, None], 0.0),
            axis=1,
        )
    upper_part = combine.astype(jnp.bfloat16)
    lower_part = (combine - upper_part.astype(jnp.float32)).astype(jnp.bfloat16)
    token_count = weights.shape[0]
    both = jnp.dot(
        jnp.concatenate([upper_part, lower_part], axis=0),
        gathered,
        preferred_element_type=jnp.float32,
    )
    return both[:token_count] + both[token_count:]


def on_device(
    layer_hidden_input,
    norm_scale_vector,
    expert_choice_index,
    expert_choice_weight,
    request_of_token,
    adapter_of_request,
    adapter_of_slot,
    expert_gate_up_weight,
    expert_down_weight,
    adapter_down_weight,
    adapter_up_weight,
):
    tok_rows, model_width = layer_hidden_input.shape
    top_count = expert_choice_index.shape[1]
    pg_size = lax.axis_size(PG_AXES)
    expert_count = pg_size // 2
    slot_cap = 4 * tok_rows * top_count // (3 * expert_count)
    half_width = model_width // lax.axis_size("kv")
    kv_index = lax.axis_index("kv")
    normalized_input = normalize(layer_hidden_input, norm_scale_vector)
    own_features = lax.dynamic_slice_in_dim(normalized_input, kv_index * half_width, half_width, axis=1)
    down_own = lax.dynamic_slice_in_dim(adapter_down_weight[0], kv_index * half_width, half_width, axis=0)
    rank_half = down_own.shape[1]
    packed = jnp.concatenate([down_own.T, adapter_up_weight[0]], axis=0)
    flat_ids = expert_choice_index.reshape(-1)
    slot_rank = rank_in_expert(flat_ids, expert_count)
    rank_table = slot_rank.reshape(tok_rows, top_count)
    first_slot = 2 * expert_choice_index * slot_cap + rank_table
    second_slot = first_slot + slot_cap
    slot_total = pg_size * slot_cap
    outbox = place_rows((first_slot, second_slot), slot_total, own_features).reshape(
        pg_size, slot_cap, half_width
    )
    inbox_half = lax.all_to_all(outbox, PG_AXES, split_axis=0, concat_axis=0, tiled=True)
    packed_all = lax.all_gather(packed, PG_AXES, axis=0, tiled=False)
    weights = split_weights(expert_gate_up_weight, expert_down_weight, half_width)
    inbox_half, packed_all, weights = lax.optimization_barrier((inbox_half, packed_all, weights))
    half_out = expert_half(inbox_half.reshape(pg_size * slot_cap, half_width), weights)
    results = lax.all_to_all(
        half_out.reshape(pg_size, slot_cap, half_width),
        PG_AXES,
        split_axis=0,
        concat_axis=0,
        tiled=True,
    )
    moe_sum = collect_rows(
        (first_slot, second_slot),
        slot_total,
        expert_choice_weight,
        results.reshape(slot_total, half_width),
    )
    request_count = adapter_of_request.shape[0]
    owner_table = request_of_token[:, None] == jnp.arange(request_count, dtype=jnp.int32)[None, :]
    token_adapter = jnp.sum(jnp.where(owner_table, adapter_of_request[None, :], 0), axis=1)
    slot_count = packed_all.shape[0]
    down_all = packed_all[:, 0:rank_half, :].reshape(slot_count * rank_half, half_width)
    up_all = packed_all[:, rank_half:, :].reshape(slot_count * rank_half, half_width)
    partial_rank = lax.dot_general(
        own_features, down_all, (((1,), (1,)), ((), ())), preferred_element_type=jnp.float32
    )
    rank_projected = lax.psum(partial_rank, "kv").reshape(tok_rows, slot_count, rank_half)
    matched = adapter_of_slot[None, :, None] == token_adapter[:, None, None]
    rank_projected = jnp.where(matched, rank_projected, 0.0).astype(jnp.bfloat16)
    flat_low = rank_projected.reshape(tok_rows, slot_count * rank_half)
    adapter_total_output = jnp.dot(flat_low, up_all, preferred_element_type=jnp.float32)
    return (moe_sum + adapter_total_output).astype(jnp.bfloat16)


def solution(mesh):
    kv_count = mesh.shape["kv"]
    pg_count = mesh.shape["pg"]
    y_count = 4 if pg_count % 4 == 0 else 1
    rest = pg_count // y_count
    z_count = 8 if rest % 8 == 0 else rest
    x_count = rest // z_count
    split_mesh = jax.sharding.Mesh(
        mesh.devices.reshape(kv_count, x_count, z_count, y_count), ("kv",) + PG_AXES
    )
    pg = PG_AXES
    placed = (
        P(pg, None),
        P(),
        P(pg, None),
        P(pg, None),
        P(pg),
        P(),
        P(),
        P(pg, None, None, "kv"),
        P(pg, "kv", None),
        P(pg, None, None),
        P(pg, None, "kv"),
    )
    return jax.shard_map(
        on_device, mesh=split_mesh, in_specs=placed, out_specs=P(pg, "kv"), check_vma=False
    )
```
